128 devices in a mesh: dev: 128 (over z, y, x, core).
Axes of the slice: x: 4, y: 4, z: 4, core: 2. Of those that a mesh axis runs over, the one named last changes fastest.
Arguments:
- prior_trajectories: bfloat16 [128, 256, 1536], P('dev'), may hold values from -6 to 6
- output_linear_operator: bfloat16 [1536, 24], replicated, may hold values from -0.15625 to 0.15625
- recorded_output: float32 [2, 256, 24], replicated, may hold values from -6 to 6
- sensor_noise_spread: float32 [2, 256], replicated, may hold values from 0.5 to 4
- nearby_rotor_positions: int32 [128, 128], replicated, may hold values from 0 to 255, as said below
- cutoff_listing_amounts: int32 [128, 2], replicated, may hold values from 16 to 128, as said below
Outputs:
- analysis: bfloat16 [128, 256, 1536], P('dev')
The draws below stay inside these ranges and needn't reach their ends.
Inputs may be any that keep to these rules, and one draw needn't show every extreme that they name: `nearby_rotor_positions`: row b lists turbines within 8 positions of block b's first turbine b * 2 (cyclically), nearest first; entries may repeat. `cutoff_listing_amounts`: column 0 (short radius) is at most 64 and column 1 (long radius) at least 64; some block has 64 in column 0 and some block has 128 in column 1.
All inputs are finite; a program needn't handle non-finite values.
Results may differ from the reference program's by a relative error of at most 0.012.
Values may be sent and summed in bfloat16 or wider, within the bound.
No kernel may reach another device: no remote copies, remote signals or barrier semaphores. Data moves between devices by JAX's collectives and lax.ppermute only.
A program may use at most 64 MiB of HBM per device.

```python
import math
import jax
import jax.numpy as jnp
from jax import lax

MEMBERS_IN_SET = 128
S = 24
BT = 2
HMAX = 128
NSI = 6
TURB_DEV = 2
FEATURE_NUMBER = 1536
ROTOR_NUMBER = 256
NB = 128


def draw_nearby_rotor_positions(key, part):
    offsets = jax.random.randint(key, (NB, HMAX), -4 * TURB_DEV, 4 * TURB_DEV + 1)
    ranking = jnp.argsort(jnp.abs(offsets), axis=1, stable=True)
    nearest = jnp.take_along_axis(offsets, ranking, axis=1)
    anchor = jnp.arange(NB, dtype=jnp.int32)[:, None] * BT
    return jnp.mod(anchor + nearest, ROTOR_NUMBER).astype(jnp.int32)


def draw_cutoff_listing_amounts(key, part):
    key_short = jax.random.fold_in(key, 11)
    key_long = jax.random.fold_in(key, 12)
    key_first = jax.random.fold_in(key, 13)
    key_second = jax.random.fold_in(key, 14)
    short_count = jax.random.randint(key_short, (NB,), HMAX // 8, HMAX // 2 + 1)
    long_count = jax.random.randint(key_long, (NB,), HMAX // 2, HMAX + 1)
    short_count = short_count.at[jax.random.randint(key_first, (), 0, NB)].set(HMAX // 2)
    long_count = long_count.at[jax.random.randint(key_second, (), 0, NB)].set(HMAX)
    return jnp.stack([short_count, long_count], axis=1).astype(jnp.int32)


def levels(own_key, extent, cuts, least, largest):
    gain = 1.0
    for dim, shards_of in cuts:
        heights = jax.random.uniform(jax.random.fold_in(jax.random.fold_in(own_key, 6), dim), (shards_of,), jnp.float32, least / len(cuts), largest / len(cuts))
        gain = gain * jnp.repeat(jnp.exp(heights), extent[dim] // shards_of).reshape((-1,) + (1,) * (len(extent) - 1 - dim))
    return gain


def noise(key, dims, scale, bound, cuts=(), kind=jnp.bfloat16):
    entries = scale * jax.random.normal(key, dims, jnp.float32)
    if cuts:
        entries = entries * levels(key, dims, cuts, -0.22, 0.18)
    return jnp.clip(entries, -bound, bound).astype(kind)


def setup_inputs(seed: int = 0) -> dict:
    key_of = jax.random.split(jax.random.key(seed), 7)
    return {
        "prior_trajectories": noise(key_of[0], (MEMBERS_IN_SET, ROTOR_NUMBER, FEATURE_NUMBER), 1.0, 6.0, ((0, 128),)),
        "output_linear_operator": noise(key_of[1], (FEATURE_NUMBER, S), FEATURE_NUMBER ** -0.5, 0.15625),
        "recorded_output": noise(key_of[2], (2, ROTOR_NUMBER, S), 1.0, 6.0, (), jnp.float32),
        "sensor_noise_spread": jnp.clip(jnp.exp(jax.random.uniform(key_of[3], (2, ROTOR_NUMBER), jnp.float32, math.log(0.5), math.log(4.0))), 0.5, 4.0),
        "nearby_rotor_positions": draw_nearby_rotor_positions(jax.random.fold_in(key_of[6], 71), 0),
        "cutoff_listing_amounts": draw_cutoff_listing_amounts(jax.random.fold_in(key_of[6], 71), 0),
    }


def observe(states, output_linear_operator):
    flat = states.reshape(-1, states.shape[-1])
    values = jnp.dot(flat, output_linear_operator, preferred_element_type=jnp.float32)
    return values.astype(jnp.bfloat16).reshape(states.shape[:-1] + (output_linear_operator.shape[1],))

def block_weights(halo_values, halo_turbines, counts, observed_now, error_now):
    members = halo_values.shape[0]
    blocks = halo_values.shape[1]
    width = halo_values.shape[2]
    position = jnp.arange(width, dtype=jnp.float32)[None, :]
    limit = counts.astype(jnp.float32)[:, None]
    taper = jnp.where(position < limit, (1.0 - position / limit) ** 2, 0.0)
    weighting = (taper / error_now[halo_turbines])[:, :, None]
    values = halo_values.astype(jnp.float32)
    center = lax.optimization_barrier(jnp.mean(values, axis=0))
    spread = values - center
    innovation = observed_now[halo_turbines] - center
    weighted = spread * weighting
    flat_spread = spread.reshape(members, blocks, -1)
    flat_weighted = weighted.reshape(members, blocks, -1)
    gram = jnp.einsum('kbm,lbm->bkl', flat_weighted, flat_spread, precision=lax.Precision.HIGHEST)
    identity = jnp.eye(members, dtype=jnp.float32)
    system = (members - 1) * identity + gram
    scale = jnp.sqrt(lax.optimization_barrier(jnp.sum(system * system, axis=(1, 2))))
    root = system / scale[:, None, None]
    inverse = jnp.broadcast_to(identity, system.shape)
    for sweep in range(NSI):
        middle = 1.5 * identity - 0.5 * jnp.einsum('bkl,blm->bkm', inverse, root, precision=lax.Precision.HIGHEST)
        root = jnp.einsum('bkl,blm->bkm', root, middle, precision=lax.Precision.HIGHEST)
        inverse = jnp.einsum('bkl,blm->bkm', middle, inverse, precision=lax.Precision.HIGHEST)
    inverse_root = inverse / jnp.sqrt(scale)[:, None, None]
    pull = jnp.einsum('kbm,bm->bk', flat_weighted, innovation.reshape(blocks, -1), precision=lax.Precision.HIGHEST)
    halfway = jnp.einsum('bkl,bl->bk', inverse_root, pull, precision=lax.Precision.HIGHEST)
    offset = jnp.einsum('bkl,bl->bk', inverse_root, halfway, precision=lax.Precision.HIGHEST)
    return math.sqrt(members - 1) * inverse_root + offset[:, :, None]

def apply_weights(rows, weights):
    values = rows.astype(jnp.float32)
    center = lax.optimization_barrier(jnp.mean(values, axis=0))
    spread = values - center
    moved = jnp.einsum('bik,ibm->kbm', weights, spread, precision=lax.Precision.HIGHEST)
    return (center + moved).astype(jnp.bfloat16)

def perform_sample_analysis(states, output_linear_operator, observed_now, error_now, nearby_rotor_positions, counts):
    members, rotor_vectors, rotor_line = states.shape
    values = observe(states, output_linear_operator)
    blocks = nearby_rotor_positions.shape[0]
    group = math.gcd(blocks, 16)

    def one_group(first):
        halo_turbines = lax.dynamic_slice_in_dim(nearby_rotor_positions, first, group, 0)
        group_counts = lax.dynamic_slice_in_dim(counts, first, group, 0)
        halo_values = jnp.take(values, halo_turbines.reshape(-1), axis=1).reshape(members, group, -1, values.shape[2])
        weights = block_weights(halo_values, halo_turbines, group_counts, observed_now, error_now)
        rows = lax.dynamic_slice_in_dim(states, (first * BT).astype(jnp.int32), group * BT, 1)
        return apply_weights(rows.reshape(members, group, BT * rotor_line), weights)
    starts = jnp.arange(0, blocks, group, dtype=jnp.int32)
    pieces = lax.map(one_group, starts)
    return jnp.transpose(pieces, (1, 0, 2, 3)).reshape(members, rotor_vectors, rotor_line)

def reference(prior_trajectories, output_linear_operator, recorded_output, sensor_noise_spread, nearby_rotor_positions, cutoff_listing_amounts):
    between_analyses_vector = perform_sample_analysis(prior_trajectories, output_linear_operator, recorded_output[0], sensor_noise_spread[0], nearby_rotor_positions, cutoff_listing_amounts[:, 0])
    return perform_sample_analysis(between_analyses_vector, output_linear_operator, recorded_output[1], sensor_noise_spread[1], nearby_rotor_positions, cutoff_listing_amounts[:, 1])
```

```python
import math

import jax
import jax.numpy as jnp
from jax import lax
from jax.sharding import PartitionSpec as P

NSI = 6
HALO_REACH = 8


def block_weights(window, taper_bins, observed_window):
    members = window.shape[0]
    values = window.astype(jnp.float32)
    center = jnp.mean(values, axis=0)
    spread = values - center
    innovation = observed_window - center
    weighted = spread * taper_bins[None, :, None]
    flat_spread = spread.reshape(members, -1)
    flat_weighted = weighted.reshape(members, -1)
    gram = jnp.einsum("km,lm->kl", flat_weighted, flat_spread, precision=lax.Precision.HIGHEST)
    identity = jnp.eye(members, dtype=jnp.float32)
    system = (members - 1) * identity + gram
    scale = jnp.sqrt(jnp.sum(system * system))
    root = system / scale
    inverse = identity
    for sweep in range(NSI):
        middle = 1.5 * identity - 0.5 * jnp.dot(inverse, root, precision=lax.Precision.HIGHEST)
        root = jnp.dot(root, middle, precision=lax.Precision.HIGHEST)
        inverse = jnp.dot(middle, inverse, precision=lax.Precision.HIGHEST)
    inverse_root = inverse / jnp.sqrt(scale)
    pull = jnp.dot(flat_weighted, innovation.reshape(-1), precision=lax.Precision.HIGHEST)
    halfway = jnp.dot(inverse_root, pull, precision=lax.Precision.HIGHEST)
    offset = jnp.dot(inverse_root, halfway, precision=lax.Precision.HIGHEST)
    return math.sqrt(members - 1) * inverse_root + offset[:, None]


def apply_weights(rows, weights):
    values = rows.astype(jnp.float32)
    center = jnp.mean(values, axis=0)
    spread = values - center
    moved = jnp.einsum("ik,im->km", weights, spread, precision=lax.Precision.HIGHEST)
    return (center + moved).astype(jnp.bfloat16)


def on_device(
    prior_trajectories,
    output_linear_operator,
    recorded_output,
    sensor_noise_spread,
    nearby_rotor_positions,
    cutoff_listing_amounts,
):
    _, rotor_vectors, rotor_line = prior_trajectories.shape
    blocks, width = nearby_rotor_positions.shape
    devices = lax.axis_size("dev")
    block_turbines = rotor_vectors // blocks
    members = devices
    steps_count = output_linear_operator.shape[1]
    me = lax.axis_index("dev")
    first_turbine = me * block_turbines
    reach_blocks = -(-HALO_REACH // block_turbines)
    offsets = list(range(-reach_blocks, reach_blocks + 1))
    window_turbines = len(offsets) * block_turbines
    window_first = first_turbine - reach_blocks * block_turbines

    own_halo = lax.dynamic_index_in_dim(nearby_rotor_positions, me, 0, keepdims=False)
    own_counts = lax.dynamic_index_in_dim(cutoff_listing_amounts, me, 0, keepdims=False)
    window_ids = jnp.mod(window_first + jnp.arange(window_turbines, dtype=jnp.int32), rotor_vectors)
    relative = jnp.mod(own_halo - window_first, rotor_vectors)
    bins = (relative[:, None] == jnp.arange(window_turbines, dtype=jnp.int32)[None, :]).astype(
        jnp.float32
    )
    position = jnp.arange(width, dtype=jnp.float32)

    def taper_of(which):
        limit = own_counts[which].astype(jnp.float32)
        taper = jnp.where(position < limit, (1.0 - position / limit) ** 2, 0.0)
        weighting = taper / jnp.take(sensor_noise_spread[which], own_halo, axis=0)
        return jnp.sum(bins * weighting[:, None], axis=0)

    def observe_rows(rows):
        flat = rows.reshape(-1, rotor_line)
        values = jnp.dot(flat, output_linear_operator, preferred_element_type=jnp.float32)
        return values.astype(jnp.bfloat16).reshape(members, block_turbines, steps_count)

    def gather_window(own):
        pieces = []
        for o in offsets:
            if o == 0:
                pieces.append(own)
            else:
                pairs = [((d + o) % devices, d) for d in range(devices)]
                pieces.append(lax.ppermute(own, "dev", pairs))
        return jnp.concatenate(pieces, axis=1)

    def analysis(rows, which):
        own = observe_rows(rows)
        window = gather_window(own)
        observed_window = jnp.take(recorded_output[which], window_ids, axis=0)
        weights = block_weights(window, taper_of(which), observed_window)
        flat_rows = rows.reshape(members, block_turbines * rotor_line)
        return apply_weights(flat_rows, weights).reshape(members, block_turbines, rotor_line)

    split = prior_trajectories.reshape(devices, block_turbines, rotor_line)
    rows0 = lax.all_to_all(split, "dev", split_axis=0, concat_axis=0, tiled=True)
    rows1 = analysis(rows0, 0)
    rows2 = analysis(rows1, 1)
    back = lax.all_to_all(rows2, "dev", split_axis=0, concat_axis=0, tiled=True)
    return back.reshape(1, rotor_vectors, rotor_line)


def solution(mesh):
    return jax.shard_map(
        on_device,
        mesh=mesh,
        in_specs=(P("dev", None, None), P(), P(), P(), P(), P()),
        out_specs=P("dev", None, None),
        check_vma=False,
    )
```

```python
import math

import jax
import jax.numpy as jnp
from jax import lax
from jax.sharding import PartitionSpec as P

NSI = 6
HALO_REACH = 8


def block_weights(window, taper_bins, observed_window):
    members = window.shape[0]
    values = window.astype(jnp.float32)
    center = jnp.mean(values, axis=0)
    spread = values - center
    innovation = observed_window - center
    weighted = spread * taper_bins[None, :, None]
    flat_spread = spread.reshape(members, -1)
    flat_weighted = weighted.reshape(members, -1)
    gram = jnp.einsum("km,lm->kl", flat_weighted, flat_spread, precision=lax.Precision.HIGHEST)
    identity = jnp.eye(members, dtype=jnp.float32)
    system = (members - 1) * identity + gram
    scale = jnp.sqrt(jnp.sum(system * system))
    root = system / scale
    inverse = identity
    for sweep in range(NSI):
        middle = 1.5 * identity - 0.5 * jnp.dot(inverse, root, precision=lax.Precision.HIGHEST)
        root = jnp.dot(root, middle, precision=lax.Precision.HIGHEST)
        inverse = jnp.dot(middle, inverse, precision=lax.Precision.HIGHEST)
    inverse_root = inverse / jnp.sqrt(scale)
    pull = jnp.dot(flat_weighted, innovation.reshape(-1), precision=lax.Precision.HIGHEST)
    halfway = jnp.dot(inverse_root, pull, precision=lax.Precision.HIGHEST)
    offset = jnp.dot(inverse_root, halfway, precision=lax.Precision.HIGHEST)
    return math.sqrt(members - 1) * inverse_root + offset[:, None]


def apply_weights(rows, weights):
    values = rows.astype(jnp.float32)
    center = jnp.mean(values, axis=0)
    spread = values - center
    moved = jnp.einsum("ik,im->km", weights, spread, precision=lax.Precision.HIGHEST)
    return (center + moved).astype(jnp.bfloat16)


def on_device(
    prior_trajectories,
    output_linear_operator,
    recorded_output,
    sensor_noise_spread,
    nearby_rotor_positions,
    cutoff_listing_amounts,
):
    _, rotor_vectors, rotor_line = prior_trajectories.shape
    blocks, width = nearby_rotor_positions.shape
    devices = lax.axis_size("dev")
    block_turbines = rotor_vectors // blocks
    members = devices
    steps_count = output_linear_operator.shape[1]
    me = lax.axis_index("dev")
    first_turbine = me * block_turbines
    reach_blocks = -(-HALO_REACH // block_turbines)
    offsets = list(range(-reach_blocks, reach_blocks + 1))
    window_turbines = len(offsets) * block_turbines
    window_first = first_turbine - reach_blocks * block_turbines

    own_halo = lax.dynamic_index_in_dim(nearby_rotor_positions, me, 0, keepdims=False)
    own_counts = lax.dynamic_index_in_dim(cutoff_listing_amounts, me, 0, keepdims=False)
    window_ids = jnp.mod(window_first + jnp.arange(window_turbines, dtype=jnp.int32), rotor_vectors)
    relative = jnp.mod(own_halo - window_first, rotor_vectors)
    bins = (relative[:, None] == jnp.arange(window_turbines, dtype=jnp.int32)[None, :]).astype(
        jnp.float32
    )
    position = jnp.arange(width, dtype=jnp.float32)

    def taper_of(which):
        limit = own_counts[which].astype(jnp.float32)
        taper = jnp.where(position < limit, (1.0 - position / limit) ** 2, 0.0)
        weighting = taper / jnp.take(sensor_noise_spread[which], own_halo, axis=0)
        return jnp.sum(bins * weighting[:, None], axis=0)

    def observe_rows(rows):
        flat = rows.reshape(-1, rotor_line)
        values = jnp.dot(flat, output_linear_operator, preferred_element_type=jnp.float32)
        return values.astype(jnp.bfloat16).reshape(members, block_turbines, steps_count)

    def gather_window(own):
        pieces = []
        for o in offsets:
            if o == 0:
                pieces.append(own)
            else:
                pairs = [((d + o) % devices, d) for d in range(devices)]
                pieces.append(lax.ppermute(own, "dev", pairs))
        return jnp.concatenate(pieces, axis=1)

    def analysis(rows, which, window=None):
        if window is None:
            window = gather_window(observe_rows(rows))
        observed_window = jnp.take(recorded_output[which], window_ids, axis=0)
        weights = block_weights(window, taper_of(which), observed_window)
        flat_rows = rows.reshape(members, block_turbines * rotor_line)
        return apply_weights(flat_rows, weights).reshape(members, block_turbines, rotor_line)

    member_values = jnp.dot(
        prior_trajectories.reshape(rotor_vectors, rotor_line),
        output_linear_operator,
        preferred_element_type=jnp.float32,
    ).astype(jnp.bfloat16)
    lead = reach_blocks * block_turbines
    tail = window_turbines - lead
    extended = jnp.concatenate(
        [member_values[rotor_vectors - lead :], member_values, member_values[: tail - block_turbines]],
        axis=0,
    ).reshape(-1, block_turbines, steps_count)
    cut = jnp.stack([extended[k : k + blocks] for k in range(len(offsets))], axis=1)
    cut = cut.reshape(devices, window_turbines, steps_count)
    window0 = lax.all_to_all(cut, "dev", split_axis=0, concat_axis=0, tiled=True)
    split = prior_trajectories.reshape(devices, block_turbines, rotor_line)
    rows0 = lax.all_to_all(split, "dev", split_axis=0, concat_axis=0, tiled=True)
    rows1 = analysis(rows0, 0, window0)
    rows2 = analysis(rows1, 1)
    back = lax.all_to_all(rows2, "dev", split_axis=0, concat_axis=0, tiled=True)
    return back.reshape(1, rotor_vectors, rotor_line)


def solution(mesh):
    return jax.shard_map(
        on_device,
        mesh=mesh,
        in_specs=(P("dev", None, None), P(), P(), P(), P(), P()),
        out_specs=P("dev", None, None),
        check_vma=False,
    )
```

```python
import math

import jax
import jax.numpy as jnp
from jax import lax
from jax.sharding import PartitionSpec as P

NSI = 6
HALO_REACH = 8


def block_weights(window, taper_bins, observed_window):
    members = window.shape[0]
    values = window.astype(jnp.float32)
    center = jnp.mean(values, axis=0)
    spread = values - center
    innovation = observed_window - center
    weighted = spread * taper_bins[None, :, None]
    flat_spread = spread.reshape(members, -1)
    flat_weighted = weighted.reshape(members, -1)
    gram = jnp.einsum("km,lm->kl", flat_weighted, flat_spread, precision=lax.Precision.HIGHEST)
    identity = jnp.eye(members, dtype=jnp.float32)
    system = (members - 1) * identity + gram
    scale = jnp.sqrt(jnp.sum(system * system))
    root = system / scale
    inverse = identity
    for sweep in range(NSI):
        middle = 1.5 * identity - 0.5 * jnp.dot(inverse, root, precision=lax.Precision.HIGHEST)
        root = jnp.dot(root, middle, precision=lax.Precision.HIGHEST)
        inverse = jnp.dot(middle, inverse, precision=lax.Precision.HIGHEST)
    inverse_root = inverse / jnp.sqrt(scale)
    pull = jnp.dot(flat_weighted, innovation.reshape(-1), precision=lax.Precision.HIGHEST)
    halfway = jnp.dot(inverse_root, pull, precision=lax.Precision.HIGHEST)
    offset = jnp.dot(inverse_root, halfway, precision=lax.Precision.HIGHEST)
    return math.sqrt(members - 1) * inverse_root + offset[:, None]


def apply_weights(rows, weights):
    values = rows.astype(jnp.float32)
    center = jnp.mean(values, axis=0)
    spread = values - center
    moved = jnp.einsum("ik,im->km", weights, spread, precision=lax.Precision.HIGHEST)
    return (center + moved).astype(jnp.bfloat16)


def on_device(
    prior_trajectories,
    output_linear_operator,
    recorded_output,
    sensor_noise_spread,
    nearby_rotor_positions,
    cutoff_listing_amounts,
):
    _, rotor_vectors, rotor_line = prior_trajectories.shape
    blocks, width = nearby_rotor_positions.shape
    devices = lax.axis_size("dev")
    block_turbines = rotor_vectors // blocks
    members = devices
    steps_count = output_linear_operator.shape[1]
    me = lax.axis_index("dev")
    first_turbine = me * block_turbines
    reach_blocks = -(-HALO_REACH // block_turbines)
    offsets = list(range(-reach_blocks, reach_blocks + 1))
    window_turbines = len(offsets) * block_turbines
    window_first = first_turbine - reach_blocks * block_turbines

    own_halo = lax.dynamic_index_in_dim(nearby_rotor_positions, me, 0, keepdims=False)
    own_counts = lax.dynamic_index_in_dim(cutoff_listing_amounts, me, 0, keepdims=False)
    window_ids = jnp.mod(window_first + jnp.arange(window_turbines, dtype=jnp.int32), rotor_vectors)
    relative = jnp.mod(own_halo - window_first, rotor_vectors)
    bins = (relative[:, None] == jnp.arange(window_turbines, dtype=jnp.int32)[None, :]).astype(
        jnp.float32
    )
    position = jnp.arange(width, dtype=jnp.float32)

    def taper_of(which):
        limit = own_counts[which].astype(jnp.float32)
        taper = jnp.where(position < limit, (1.0 - position / limit) ** 2, 0.0)
        weighting = taper / jnp.take(sensor_noise_spread[which], own_halo, axis=0)
        return jnp.sum(bins * weighting[:, None], axis=0)

    def observe_rows(rows):
        flat = rows.reshape(-1, rotor_line)
        values = jnp.dot(flat, output_linear_operator, preferred_element_type=jnp.float32)
        return values.astype(jnp.bfloat16).reshape(members, block_turbines, steps_count)

    def gather_window(own):
        pieces = []
        for o in offsets:
            if o == 0:
                pieces.append(own)
            else:
                pairs = [((d + o) % devices, d) for d in range(devices)]
                pieces.append(lax.ppermute(own, "dev", pairs))
        return jnp.concatenate(pieces, axis=1)

    def analysis(rows, which, window=None):
        if window is None:
            window = gather_window(observe_rows(rows))
        observed_window = jnp.take(recorded_output[which], window_ids, axis=0)
        weights = block_weights(window, taper_of(which), observed_window)
        flat_rows = rows.reshape(members, block_turbines * rotor_line)
        return apply_weights(flat_rows, weights).reshape(members, block_turbines, rotor_line)

    member_values = jnp.dot(
        prior_trajectories.reshape(rotor_vectors, rotor_line),
        output_linear_operator,
        preferred_element_type=jnp.float32,
    ).astype(jnp.bfloat16)
    lead = reach_blocks * block_turbines
    tail = window_turbines - lead
    extended = jnp.concatenate(
        [member_values[rotor_vectors - lead :], member_values, member_values[: tail - block_turbines]],
        axis=0,
    ).reshape(-1, block_turbines, steps_count)
    cut = jnp.stack([extended[k : k + blocks] for k in range(len(offsets))], axis=1)
    half = window_turbines * steps_count // block_turbines
    padded = -(-(rotor_line + half) // 128) * 128
    cut = cut.reshape(devices, block_turbines, half)
    split = prior_trajectories.reshape(devices, block_turbines, rotor_line)
    payload = jnp.concatenate(
        [split, cut, jnp.zeros((devices, block_turbines, padded - rotor_line - half), jnp.bfloat16)],
        axis=2,
    )
    arrived = lax.all_to_all(payload, "dev", split_axis=0, concat_axis=0, tiled=True)
    rows0 = arrived[:, :, :rotor_line]
    window0 = arrived[:, :, rotor_line : rotor_line + half].reshape(members, window_turbines, steps_count)
    rows1 = analysis(rows0, 0, window0)
    rows2 = analysis(rows1, 1)
    back = lax.all_to_all(rows2, "dev", split_axis=0, concat_axis=0, tiled=True)
    return back.reshape(1, rotor_vectors, rotor_line)


def solution(mesh):
    return jax.shard_map(
        on_device,
        mesh=mesh,
        in_specs=(P("dev", None, None), P(), P(), P(), P(), P()),
        out_specs=P("dev", None, None),
        check_vma=False,
    )
```

```python
import math

import jax
import jax.numpy as jnp
from jax import lax
from jax.experimental import pallas as pl
from jax.experimental.pallas import tpu as pltpu
from jax.sharding import PartitionSpec as P

NSI = 6
HI = lax.Precision.HIGHEST
HALO_REACH = 8


def transform_kernel(spread_ref, taper_ref, innovation_ref, out_ref):
    members = spread_ref.shape[0]
    nt = (((1,), (1,)), ((), ()))
    spread = spread_ref[...]
    weighted = spread * taper_ref[...]
    gram = lax.dot_general(weighted, spread, nt, precision=HI, preferred_element_type=jnp.float32)
    rows = lax.broadcasted_iota(jnp.int32, (members, members), 0)
    cols = lax.broadcasted_iota(jnp.int32, (members, members), 1)
    identity = (rows == cols).astype(jnp.float32)
    system = (members - 1) * identity + gram
    scale = jnp.sqrt(jnp.sum(system * system))
    root = system / scale
    inverse = identity
    for sweep in range(NSI):
        middle = 1.5 * identity - 0.5 * jnp.dot(inverse, root, precision=HI, preferred_element_type=jnp.float32)
        root = jnp.dot(root, middle, precision=HI, preferred_element_type=jnp.float32)
        inverse = jnp.dot(middle, inverse, precision=HI, preferred_element_type=jnp.float32)
    inverse_root = inverse / jnp.sqrt(scale)
    pull = lax.dot_general(innovation_ref[...], weighted, nt, precision=HI, preferred_element_type=jnp.float32)
    halfway = lax.dot_general(pull, inverse_root, nt, precision=HI, preferred_element_type=jnp.float32)
    offset = lax.dot_general(inverse_root, halfway, nt, precision=HI, preferred_element_type=jnp.float32)
    out_ref[...] = math.sqrt(members - 1) * inverse_root + offset[:, 0:1]


def block_weights(window, taper_bins, observed_window):
    members, turbines, steps = window.shape
    values = window.astype(jnp.float32)
    center = jnp.mean(values, axis=0)
    spread = (values - center).reshape(members, -1)
    innovation = (observed_window - center).reshape(1, -1)
    taper = jnp.broadcast_to(taper_bins[:, None], (turbines, steps)).reshape(1, -1)
    width = spread.shape[1]
    lanes = -(-width // 128) * 128
    spread = jnp.pad(spread, ((0, 0), (0, lanes - width)))
    taper = jnp.pad(taper, ((0, 0), (0, lanes - width)))
    innovation = jnp.pad(innovation, ((0, 7), (0, lanes - width)))
    vmem = pl.BlockSpec(memory_space=pltpu.VMEM)
    return pl.pallas_call(
        transform_kernel,
        out_shape=jax.ShapeDtypeStruct((members, members), jnp.float32),
        in_specs=[vmem, vmem, vmem],
        out_specs=vmem,
    )(spread, taper, innovation)


def apply_weights(rows, weights):
    values = rows.astype(jnp.float32)
    center = jnp.mean(values, axis=0)
    spread = values - center
    moved = jnp.einsum("ik,im->km", weights, spread, precision=lax.Precision.HIGHEST)
    return (center + moved).astype(jnp.bfloat16)


def on_device(
    prior_trajectories,
    output_linear_operator,
    recorded_output,
    sensor_noise_spread,
    nearby_rotor_positions,
    cutoff_listing_amounts,
):
    _, rotor_vectors, rotor_line = prior_trajectories.shape
    blocks, width = nearby_rotor_positions.shape
    devices = lax.axis_size("dev")
    block_turbines = rotor_vectors // blocks
    members = devices
    steps_count = output_linear_operator.shape[1]
    me = lax.axis_index("dev")
    first_turbine = me * block_turbines
    reach_blocks = -(-HALO_REACH // block_turbines)
    offsets = list(range(-reach_blocks, reach_blocks + 1))
    window_turbines = len(offsets) * block_turbines
    window_first = first_turbine - reach_blocks * block_turbines

    own_halo = lax.dynamic_index_in_dim(nearby_rotor_positions, me, 0, keepdims=False)
    own_counts = lax.dynamic_index_in_dim(cutoff_listing_amounts, me, 0, keepdims=False)
    window_ids = jnp.mod(window_first + jnp.arange(window_turbines, dtype=jnp.int32), rotor_vectors)
    relative = jnp.mod(own_halo - window_first, rotor_vectors)
    bins = (relative[:, None] == jnp.arange(window_turbines, dtype=jnp.int32)[None, :]).astype(
        jnp.float32
    )
    position = jnp.arange(width, dtype=jnp.float32)

    def taper_of(which):
        limit = own_counts[which].astype(jnp.float32)
        taper = jnp.where(position < limit, (1.0 - position / limit) ** 2, 0.0)
        weighting = taper / jnp.take(sensor_noise_spread[which], own_halo, axis=0)
        return jnp.sum(bins * weighting[:, None], axis=0)

    def observe_rows(rows):
        flat = rows.reshape(-1, rotor_line)
        values = jnp.dot(flat, output_linear_operator, preferred_element_type=jnp.float32)
        return values.astype(jnp.bfloat16).reshape(members, block_turbines, steps_count)

    def gather_window(own):
        pieces = []
        for o in offsets:
            if o == 0:
                pieces.append(own)
            else:
                pairs = [((d + o) % devices, d) for d in range(devices)]
                pieces.append(lax.ppermute(own, "dev", pairs))
        return jnp.concatenate(pieces, axis=1)

    def analysis(rows, which, window=None):
        if window is None:
            window = gather_window(observe_rows(rows))
        observed_window = jnp.take(recorded_output[which], window_ids, axis=0)
        weights = block_weights(window, taper_of(which), observed_window)
        flat_rows = rows.reshape(members, block_turbines * rotor_line)
        return apply_weights(flat_rows, weights).reshape(members, block_turbines, rotor_line)

    member_values = jnp.dot(
        prior_trajectories.reshape(rotor_vectors, rotor_line),
        output_linear_operator,
        preferred_element_type=jnp.float32,
    ).astype(jnp.bfloat16)
    lead = reach_blocks * block_turbines
    tail = window_turbines - lead
    extended = jnp.concatenate(
        [member_values[rotor_vectors - lead :], member_values, member_values[: tail - block_turbines]],
        axis=0,
    ).reshape(-1, block_turbines, steps_count)
    cut = jnp.stack([extended[k : k + blocks] for k in range(len(offsets))], axis=1)
    half = window_turbines * steps_count // block_turbines
    padded = -(-(rotor_line + half) // 128) * 128
    cut = cut.reshape(devices, block_turbines, half)
    split = prior_trajectories.reshape(devices, block_turbines, rotor_line)
    payload = jnp.concatenate(
        [split, cut, jnp.zeros((devices, block_turbines, padded - rotor_line - half), jnp.bfloat16)],
        axis=2,
    )
    arrived = lax.all_to_all(payload, "dev", split_axis=0, concat_axis=0, tiled=True)
    rows0 = arrived[:, :, :rotor_line]
    window0 = arrived[:, :, rotor_line : rotor_line + half].reshape(members, window_turbines, steps_count)
    rows1 = analysis(rows0, 0, window0)
    rows2 = analysis(rows1, 1)
    back = lax.all_to_all(rows2, "dev", split_axis=0, concat_axis=0, tiled=True)
    return back.reshape(1, rotor_vectors, rotor_line)


def solution(mesh):
    return jax.shard_map(
        on_device,
        mesh=mesh,
        in_specs=(P("dev", None, None), P(), P(), P(), P(), P()),
        out_specs=P("dev", None, None),
        check_vma=False,
    )
```

```python
import math

import jax
import jax.numpy as jnp
from jax import lax
from jax.sharding import PartitionSpec as P

NSI = 6
HALO_REACH = 8


def block_weights(window, taper_bins, observed_window):
    members = window.shape[0]
    values = window.astype(jnp.float32)
    center = jnp.mean(values, axis=0)
    spread = values - center
    innovation = observed_window - center
    weighted = spread * taper_bins[None, :, None]
    flat_spread = spread.reshape(members, -1)
    flat_weighted = weighted.reshape(members, -1)
    gram = jnp.einsum("km,lm->kl", flat_weighted, flat_spread, precision=lax.Precision.HIGHEST)
    identity = jnp.eye(members, dtype=jnp.float32)
    system = (members - 1) * identity + gram
    scale = jnp.sqrt(jnp.sum(system * system))
    root = system / scale
    inverse = identity
    for sweep in range(NSI):
        middle = 1.5 * identity - 0.5 * jnp.dot(inverse, root, precision=lax.Precision.HIGHEST)
        root = jnp.dot(root, middle, precision=lax.Precision.HIGHEST)
        inverse = jnp.dot(middle, inverse, precision=lax.Precision.HIGHEST)
    inverse_root = inverse / jnp.sqrt(scale)
    pull = jnp.dot(flat_weighted, innovation.reshape(-1), precision=lax.Precision.HIGHEST)
    halfway = jnp.dot(inverse_root, pull, precision=lax.Precision.HIGHEST)
    offset = jnp.dot(inverse_root, halfway, precision=lax.Precision.HIGHEST)
    return math.sqrt(members - 1) * inverse_root + offset[:, None]


def apply_weights(rows, weights):
    values = rows.astype(jnp.float32)
    center = jnp.mean(values, axis=0)
    spread = values - center
    moved = jnp.einsum("ik,im->km", weights, spread, precision=lax.Precision.HIGHEST)
    return (center + moved).astype(jnp.bfloat16)


def on_device(
    prior_trajectories,
    output_linear_operator,
    recorded_output,
    sensor_noise_spread,
    nearby_rotor_positions,
    cutoff_listing_amounts,
):
    _, rotor_vectors, rotor_line = prior_trajectories.shape
    blocks, width = nearby_rotor_positions.shape
    devices = lax.axis_size("dev")
    block_turbines = rotor_vectors // blocks
    members = devices
    steps_count = output_linear_operator.shape[1]
    me = lax.axis_index("dev")
    first_turbine = me * block_turbines
    reach_blocks = -(-HALO_REACH // block_turbines)
    offsets = list(range(-reach_blocks, reach_blocks + 1))
    window_turbines = len(offsets) * block_turbines
    window_first = first_turbine - reach_blocks * block_turbines

    own_halo = lax.dynamic_index_in_dim(nearby_rotor_positions, me, 0, keepdims=False)
    own_counts = lax.dynamic_index_in_dim(cutoff_listing_amounts, me, 0, keepdims=False)
    window_ids = jnp.mod(window_first + jnp.arange(window_turbines, dtype=jnp.int32), rotor_vectors)
    relative = jnp.mod(own_halo - window_first, rotor_vectors)
    bins = (relative[:, None] == jnp.arange(window_turbines, dtype=jnp.int32)[None, :]).astype(
        jnp.float32
    )
    position = jnp.arange(width, dtype=jnp.float32)

    def taper_of(which):
        limit = own_counts[which].astype(jnp.float32)
        taper = jnp.where(position < limit, (1.0 - position / limit) ** 2, 0.0)
        weighting = taper / jnp.take(sensor_noise_spread[which], own_halo, axis=0)
        return jnp.sum(bins * weighting[:, None], axis=0)

    def observe_rows(rows):
        flat = rows.reshape(-1, rotor_line)
        values = jnp.dot(flat, output_linear_operator, preferred_element_type=jnp.float32)
        return values.astype(jnp.bfloat16).reshape(members, block_turbines, steps_count)

    def gather_window(own):
        pieces = []
        for o in offsets:
            if o == 0:
                pieces.append(own)
            else:
                pairs = [((d + o) % devices, d) for d in range(devices)]
                pieces.append(lax.ppermute(own, "dev", pairs))
        return jnp.concatenate(pieces, axis=1)

    def analysis(rows, which, window=None):
        if window is None:
            window = gather_window(observe_rows(rows))
        observed_window = jnp.take(recorded_output[which], window_ids, axis=0)
        weights = block_weights(window, taper_of(which), observed_window)
        flat_rows = rows.reshape(members, block_turbines * rotor_line)
        return apply_weights(flat_rows, weights).reshape(members, block_turbines, rotor_line)

    member_values = jnp.dot(
        prior_trajectories.reshape(rotor_vectors, rotor_line),
        output_linear_operator,
        preferred_element_type=jnp.float32,
    ).astype(jnp.bfloat16)
    source = jnp.mod(
        jnp.arange(blocks, dtype=jnp.int32)[:, None] * block_turbines
        - reach_blocks * block_turbines
        + jnp.arange(window_turbines, dtype=jnp.int32)[None, :],
        rotor_vectors,
    ).reshape(-1)
    pick = (source[:, None] == jnp.arange(rotor_vectors, dtype=jnp.int32)[None, :]).astype(jnp.bfloat16)
    cut = jnp.dot(pick, member_values, preferred_element_type=jnp.float32).astype(jnp.bfloat16)
    half = window_turbines * steps_count // block_turbines
    padded = -(-(rotor_line + half) // 128) * 128
    cut = cut.reshape(devices, block_turbines, half)
    payload = jnp.pad(
        prior_trajectories.reshape(rotor_vectors, rotor_line), ((0, 0), (0, padded - rotor_line))
    ).reshape(devices, block_turbines, padded)
    payload = lax.dynamic_update_slice(payload, cut, (0, 0, rotor_line))
    arrived = lax.all_to_all(payload, "dev", split_axis=0, concat_axis=0, tiled=True)
    rows0 = arrived[:, :, :rotor_line]
    window0 = arrived[:, :, rotor_line : rotor_line + half].reshape(members, window_turbines, steps_count)
    rows1 = analysis(rows0, 0, window0)
    rows2 = analysis(rows1, 1)
    back = lax.all_to_all(rows2, "dev", split_axis=0, concat_axis=0, tiled=True)
    return back.reshape(1, rotor_vectors, rotor_line)


def solution(mesh):
    return jax.shard_map(
        on_device,
        mesh=mesh,
        in_specs=(P("dev", None, None), P(), P(), P(), P(), P()),
        out_specs=P("dev", None, None),
        check_vma=False,
    )
```

```python
import math

import jax
import jax.numpy as jnp
from jax import lax
from jax.sharding import PartitionSpec as P

NSI = 6
HALO_REACH = 8


def block_weights(window, taper_bins, observed_window):
    members = window.shape[0]
    values = window.astype(jnp.float32)
    center = jnp.mean(values, axis=0)
    spread = values - center
    innovation = observed_window - center
    weighted = spread * taper_bins[None, :, None]
    flat_spread = spread.reshape(members, -1)
    flat_weighted = weighted.reshape(members, -1)
    gram = jnp.einsum("km,lm->kl", flat_weighted, flat_spread, precision=lax.Precision.HIGHEST)
    identity = jnp.eye(members, dtype=jnp.float32)
    system = (members - 1) * identity + gram
    scale = jnp.sqrt(jnp.sum(system * system))
    root = system / scale
    inverse = identity
    for sweep in range(NSI):
        middle = 1.5 * identity - 0.5 * jnp.dot(inverse, root, precision=lax.Precision.HIGHEST)
        root = jnp.dot(root, middle, precision=lax.Precision.HIGHEST)
        inverse = jnp.dot(middle, inverse, precision=lax.Precision.HIGHEST)
    inverse_root = inverse / jnp.sqrt(scale)
    pull = jnp.dot(flat_weighted, innovation.reshape(-1), precision=lax.Precision.HIGHEST)
    halfway = jnp.dot(inverse_root, pull, precision=lax.Precision.HIGHEST)
    offset = jnp.dot(inverse_root, halfway, precision=lax.Precision.HIGHEST)
    return math.sqrt(members - 1) * inverse_root + offset[:, None]


def apply_weights(rows, weights):
    values = rows.astype(jnp.float32)
    center = jnp.mean(values, axis=0)
    spread = values - center
    moved = jnp.einsum("ik,irc->krc", weights, spread, precision=lax.Precision.HIGHEST)
    return (center + moved).astype(jnp.bfloat16)


def on_device(
    prior_trajectories,
    output_linear_operator,
    recorded_output,
    sensor_noise_spread,
    nearby_rotor_positions,
    cutoff_listing_amounts,
):
    _, rotor_vectors, rotor_line = prior_trajectories.shape
    blocks, width = nearby_rotor_positions.shape
    devices = lax.axis_size("dev")
    block_turbines = rotor_vectors // blocks
    members = devices
    steps_count = output_linear_operator.shape[1]
    me = lax.axis_index("dev")
    first_turbine = me * block_turbines
    reach_blocks = -(-HALO_REACH // block_turbines)
    offsets = list(range(-reach_blocks, reach_blocks + 1))
    window_turbines = len(offsets) * block_turbines
    window_first = first_turbine - reach_blocks * block_turbines

    own_halo = lax.dynamic_index_in_dim(nearby_rotor_positions, me, 0, keepdims=False)
    own_counts = lax.dynamic_index_in_dim(cutoff_listing_amounts, me, 0, keepdims=False)
    window_ids = jnp.mod(window_first + jnp.arange(window_turbines, dtype=jnp.int32), rotor_vectors)
    relative = jnp.mod(own_halo - window_first, rotor_vectors)
    bins = (relative[:, None] == jnp.arange(window_turbines, dtype=jnp.int32)[None, :]).astype(
        jnp.float32
    )
    position = jnp.arange(width, dtype=jnp.float32)

    def taper_of(which):
        limit = own_counts[which].astype(jnp.float32)
        taper = jnp.where(position < limit, (1.0 - position / limit) ** 2, 0.0)
        weighting = taper / jnp.take(sensor_noise_spread[which], own_halo, axis=0)
        return jnp.sum(bins * weighting[:, None], axis=0)

    def observe_rows(rows):
        values = lax.dot_general(
            rows, spread_operator, (((1, 2), (0, 1)), ((), ())), preferred_element_type=jnp.float32
        )
        return values.astype(jnp.bfloat16).reshape(members, block_turbines, steps_count)

    def gather_window(own):
        pieces = []
        for o in offsets:
            if o == 0:
                pieces.append(own)
            else:
                pairs = [((d + o) % devices, d) for d in range(devices)]
                pieces.append(lax.ppermute(own, "dev", pairs))
        return jnp.concatenate(pieces, axis=1)

    def analysis(rows, which, window=None):
        if window is None:
            window = gather_window(observe_rows(rows))
        observed_window = jnp.take(recorded_output[which], window_ids, axis=0)
        weights = block_weights(window, taper_of(which), observed_window)
        return apply_weights(rows, weights)

    member_values = jnp.dot(
        prior_trajectories.reshape(rotor_vectors, rotor_line),
        output_linear_operator,
        preferred_element_type=jnp.float32,
    ).astype(jnp.bfloat16)
    source = jnp.mod(
        jnp.arange(blocks, dtype=jnp.int32)[:, None] * block_turbines
        - reach_blocks * block_turbines
        + jnp.arange(window_turbines, dtype=jnp.int32)[None, :],
        rotor_vectors,
    ).reshape(-1)
    pick = (source[:, None] == jnp.arange(rotor_vectors, dtype=jnp.int32)[None, :]).astype(jnp.bfloat16)
    cut = jnp.dot(pick, member_values, preferred_element_type=jnp.float32).astype(jnp.bfloat16)
    lanes = 128
    tile_rows = rotor_line // lanes
    state_rows = block_turbines * tile_rows
    window_size = window_turbines * steps_count
    window_rows = -(-window_size // lanes)
    cut = jnp.pad(cut.reshape(devices, window_size), ((0, 0), (0, window_rows * lanes - window_size)))
    split = prior_trajectories.reshape(devices, state_rows, lanes)
    payload = jnp.concatenate([split, cut.reshape(devices, window_rows, lanes)], axis=1)
    arrived = lax.all_to_all(payload, "dev", split_axis=0, concat_axis=0, tiled=True)
    rows0 = arrived[:, :state_rows]
    window0 = arrived[:, state_rows:].reshape(members, window_rows * lanes)[:, :window_size]
    window0 = window0.reshape(members, window_turbines, steps_count)
    per_row = output_linear_operator.reshape(tile_rows, lanes, steps_count)
    spread_operator = jnp.stack(
        [
            jnp.pad(per_row, ((j * tile_rows, (block_turbines - 1 - j) * tile_rows), (0, 0), (0, 0)))
            for j in range(block_turbines)
        ],
        axis=2,
    )
    rows1 = analysis(rows0, 0, window0)
    rows2 = analysis(rows1, 1)
    back = lax.all_to_all(rows2, "dev", split_axis=0, concat_axis=0, tiled=True)
    return back.reshape(1, rotor_vectors, rotor_line)


def solution(mesh):
    return jax.shard_map(
        on_device,
        mesh=mesh,
        in_specs=(P("dev", None, None), P(), P(), P(), P(), P()),
        out_specs=P("dev", None, None),
        check_vma=False,
    )
```

```python
import math

import jax
import jax.numpy as jnp
from jax import lax
from jax.sharding import PartitionSpec as P

NSI = 6
HALO_REACH = 8


def block_weights(window, taper_bins, observed_window):
    members = window.shape[0]
    values = window.astype(jnp.float32)
    center = jnp.mean(values, axis=0)
    spread = values - center
    innovation = observed_window - center
    weighted = spread * taper_bins[None, :, None]
    flat_spread = spread.reshape(members, -1)
    flat_weighted = weighted.reshape(members, -1)
    gram = jnp.einsum("km,lm->kl", flat_weighted, flat_spread, precision=lax.Precision.HIGHEST)
    identity = jnp.eye(members, dtype=jnp.float32)
    system = (members - 1) * identity + gram
    scale = jnp.sqrt(jnp.sum(system * system))
    root = system / scale
    inverse = identity
    for sweep in range(NSI):
        middle = 1.5 * identity - 0.5 * jnp.dot(inverse, root, precision=lax.Precision.HIGHEST)
        root = jnp.dot(root, middle, precision=lax.Precision.HIGHEST)
        inverse = jnp.dot(middle, inverse, precision=lax.Precision.HIGHEST)
    inverse_root = inverse / jnp.sqrt(scale)
    pull = jnp.dot(flat_weighted, innovation.reshape(-1), precision=lax.Precision.HIGHEST)
    halfway = jnp.dot(inverse_root, pull, precision=lax.Precision.HIGHEST)
    offset = jnp.dot(inverse_root, halfway, precision=lax.Precision.HIGHEST)
    return math.sqrt(members - 1) * inverse_root + offset[:, None]


def apply_weights(rows, weights):
    values = rows.astype(jnp.float32)
    center = jnp.mean(values, axis=0)
    spread = values - center
    moved = jnp.einsum("ik,i...->k...", weights, spread, precision=lax.Precision.HIGHEST)
    return (center + moved).astype(jnp.bfloat16)


def on_device(
    prior_trajectories,
    output_linear_operator,
    recorded_output,
    sensor_noise_spread,
    nearby_rotor_positions,
    cutoff_listing_amounts,
):
    _, rotor_vectors, rotor_line = prior_trajectories.shape
    blocks, width = nearby_rotor_positions.shape
    devices = lax.axis_size("dev")
    block_turbines = rotor_vectors // blocks
    members = devices
    steps_count = output_linear_operator.shape[1]
    me = lax.axis_index("dev")
    first_turbine = me * block_turbines
    reach_blocks = -(-HALO_REACH // block_turbines)
    offsets = list(range(-reach_blocks, reach_blocks + 1))
    window_turbines = len(offsets) * block_turbines
    window_first = first_turbine - reach_blocks * block_turbines

    own_halo = lax.dynamic_index_in_dim(nearby_rotor_positions, me, 0, keepdims=False)
    own_counts = lax.dynamic_index_in_dim(cutoff_listing_amounts, me, 0, keepdims=False)
    window_ids = jnp.mod(window_first + jnp.arange(window_turbines, dtype=jnp.int32), rotor_vectors)
    relative = jnp.mod(own_halo - window_first, rotor_vectors)
    bins = (relative[:, None] == jnp.arange(window_turbines, dtype=jnp.int32)[None, :]).astype(
        jnp.float32
    )
    position = jnp.arange(width, dtype=jnp.float32)

    def taper_of(which):
        limit = own_counts[which].astype(jnp.float32)
        taper = jnp.where(position < limit, (1.0 - position / limit) ** 2, 0.0)
        weighting = taper / jnp.take(sensor_noise_spread[which], own_halo, axis=0)
        return jnp.sum(bins * weighting[:, None], axis=0)

    def observe_rows(rows):
        values = lax.dot_general(
            rows.reshape(members, state_rows, lanes),
            spread_operator,
            (((1, 2), (0, 1)), ((), ())),
            preferred_element_type=jnp.float32,
        )
        return values.astype(jnp.bfloat16).reshape(members, block_turbines, steps_count)

    def gather_window(own):
        pieces = []
        for o in offsets:
            if o == 0:
                pieces.append(own)
            else:
                pairs = [((d + o) % devices, d) for d in range(devices)]
                pieces.append(lax.ppermute(own, "dev", pairs))
        return jnp.concatenate(pieces, axis=1)

    def analysis(rows, which, window=None):
        if window is None:
            window = gather_window(observe_rows(rows))
        observed_window = jnp.take(recorded_output[which], window_ids, axis=0)
        weights = block_weights(window, taper_of(which), observed_window)
        return apply_weights(rows, weights)

    member_values = jnp.dot(
        prior_trajectories.reshape(rotor_vectors, rotor_line),
        output_linear_operator,
        preferred_element_type=jnp.float32,
    ).astype(jnp.bfloat16)
    source = jnp.mod(
        jnp.arange(blocks, dtype=jnp.int32)[:, None] * block_turbines
        - reach_blocks * block_turbines
        + jnp.arange(window_turbines, dtype=jnp.int32)[None, :],
        rotor_vectors,
    ).reshape(-1)
    pick = (source[:, None] == jnp.arange(rotor_vectors, dtype=jnp.int32)[None, :]).astype(jnp.bfloat16)
    cut = jnp.dot(pick, member_values, preferred_element_type=jnp.float32).astype(jnp.bfloat16)
    lanes = 128
    tile_rows = rotor_line // lanes
    state_rows = block_turbines * tile_rows
    window_size = window_turbines * steps_count
    window_rows = -(-window_size // lanes)
    cut = jnp.pad(cut.reshape(devices, window_size), ((0, 0), (0, window_rows * lanes - window_size)))
    split = prior_trajectories.reshape(devices, state_rows, lanes)
    payload = jnp.concatenate([split, cut.reshape(devices, window_rows, lanes)], axis=1)
    arrived = lax.all_to_all(payload, "dev", split_axis=0, concat_axis=0, tiled=True)
    rows0 = arrived[:, :state_rows]
    window0 = arrived[:, state_rows:].reshape(members, window_rows * lanes)[:, :window_size]
    window0 = window0.reshape(members, window_turbines, steps_count)
    per_row = output_linear_operator.reshape(tile_rows, lanes, steps_count)
    spread_operator = jnp.stack(
        [
            jnp.pad(per_row, ((j * tile_rows, (block_turbines - 1 - j) * tile_rows), (0, 0), (0, 0)))
            for j in range(block_turbines)
        ],
        axis=2,
    )
    rows1 = analysis(rows0, 0, window0)
    rows2 = analysis(rows1.reshape(members, state_rows * lanes), 1).reshape(members, block_turbines, rotor_line)
    back = lax.all_to_all(rows2, "dev", split_axis=0, concat_axis=0, tiled=True)
    return back.reshape(1, rotor_vectors, rotor_line)


def solution(mesh):
    return jax.shard_map(
        on_device,
        mesh=mesh,
        in_specs=(P("dev", None, None), P(), P(), P(), P(), P()),
        out_specs=P("dev", None, None),
        check_vma=False,
    )
```

```python
import math

import jax
import jax.numpy as jnp
from jax import lax
from jax.sharding import PartitionSpec as P

NSI = 6
HALO_REACH = 8


def block_weights(window, taper_bins, observed_window):
    members = window.shape[0]
    values = window.astype(jnp.float32)
    center = jnp.mean(values, axis=0)
    spread = values - center
    innovation = observed_window - center
    weighted = spread * taper_bins[None, :, None]
    flat_spread = spread.reshape(members, -1)
    flat_weighted = weighted.reshape(members, -1)
    gram = jnp.einsum("km,lm->kl", flat_weighted, flat_spread, precision=lax.Precision.HIGHEST)
    identity = jnp.eye(members, dtype=jnp.float32)
    system = (members - 1) * identity + gram
    scale = jnp.sqrt(jnp.sum(system * system))
    root = system / scale
    inverse = identity
    for sweep in range(NSI):
        middle = 1.5 * identity - 0.5 * jnp.dot(inverse, root, precision=lax.Precision.HIGHEST)
        both = jnp.einsum(
            "bkl,blm->bkm",
            jnp.stack([root, middle]),
            jnp.stack([middle, inverse]),
            precision=lax.Precision.HIGHEST,
        )
        root, inverse = both[0], both[1]
    inverse_root = inverse / jnp.sqrt(scale)
    pull = jnp.dot(flat_weighted, innovation.reshape(-1), precision=lax.Precision.HIGHEST)
    halfway = jnp.dot(inverse_root, pull, precision=lax.Precision.HIGHEST)
    offset = jnp.dot(inverse_root, halfway, precision=lax.Precision.HIGHEST)
    return math.sqrt(members - 1) * inverse_root + offset[:, None]


def apply_weights(rows, weights):
    values = rows.astype(jnp.float32)
    center = jnp.mean(values, axis=0)
    spread = values - center
    moved = jnp.einsum("ik,i...->k...", weights, spread, precision=lax.Precision.HIGHEST)
    return (center + moved).astype(jnp.bfloat16)


def on_device(
    prior_trajectories,
    output_linear_operator,
    recorded_output,
    sensor_noise_spread,
    nearby_rotor_positions,
    cutoff_listing_amounts,
):
    _, rotor_vectors, rotor_line = prior_trajectories.shape
    blocks, width = nearby_rotor_positions.shape
    devices = lax.axis_size("dev")
    block_turbines = rotor_vectors // blocks
    members = devices
    steps_count = output_linear_operator.shape[1]
    me = lax.axis_index("dev")
    first_turbine = me * block_turbines
    reach_blocks = -(-HALO_REACH // block_turbines)
    offsets = list(range(-reach_blocks, reach_blocks + 1))
    window_turbines = len(offsets) * block_turbines
    window_first = first_turbine - reach_blocks * block_turbines

    own_halo = lax.dynamic_index_in_dim(nearby_rotor_positions, me, 0, keepdims=False)
    own_counts = lax.dynamic_index_in_dim(cutoff_listing_amounts, me, 0, keepdims=False)
    window_ids = jnp.mod(window_first + jnp.arange(window_turbines, dtype=jnp.int32), rotor_vectors)
    relative = jnp.mod(own_halo - window_first, rotor_vectors)
    bins = (relative[:, None] == jnp.arange(window_turbines, dtype=jnp.int32)[None, :]).astype(
        jnp.float32
    )
    position = jnp.arange(width, dtype=jnp.float32)

    def taper_of(which):
        limit = own_counts[which].astype(jnp.float32)
        taper = jnp.where(position < limit, (1.0 - position / limit) ** 2, 0.0)
        weighting = taper / jnp.take(sensor_noise_spread[which], own_halo, axis=0)
        return jnp.sum(bins * weighting[:, None], axis=0)

    def observe_rows(rows):
        values = lax.dot_general(
            rows.reshape(members, state_rows, lanes),
            spread_operator,
            (((1, 2), (0, 1)), ((), ())),
            preferred_element_type=jnp.float32,
        )
        return values.astype(jnp.bfloat16).reshape(members, block_turbines, steps_count)

    def gather_window(own):
        pieces = []
        for o in offsets:
            if o == 0:
                pieces.append(own)
            else:
                pairs = [((d + o) % devices, d) for d in range(devices)]
                pieces.append(lax.ppermute(own, "dev", pairs))
        return jnp.concatenate(pieces, axis=1)

    def analysis(rows, which, window=None):
        if window is None:
            window = gather_window(observe_rows(rows))
        observed_window = jnp.take(recorded_output[which], window_ids, axis=0)
        weights = block_weights(window, taper_of(which), observed_window)
        return apply_weights(rows, weights)

    member_values = jnp.dot(
        prior_trajectories.reshape(rotor_vectors, rotor_line),
        output_linear_operator,
        preferred_element_type=jnp.float32,
    ).astype(jnp.bfloat16)
    source = jnp.mod(
        jnp.arange(blocks, dtype=jnp.int32)[:, None] * block_turbines
        - reach_blocks * block_turbines
        + jnp.arange(window_turbines, dtype=jnp.int32)[None, :],
        rotor_vectors,
    ).reshape(-1)
    pick = (source[:, None] == jnp.arange(rotor_vectors, dtype=jnp.int32)[None, :]).astype(jnp.bfloat16)
    cut = jnp.dot(pick, member_values, preferred_element_type=jnp.float32).astype(jnp.bfloat16)
    lanes = 128
    tile_rows = rotor_line // lanes
    state_rows = block_turbines * tile_rows
    window_size = window_turbines * steps_count
    window_rows = -(-window_size // lanes)
    cut = jnp.pad(cut.reshape(devices, window_size), ((0, 0), (0, window_rows * lanes - window_size)))
    split = prior_trajectories.reshape(devices, state_rows, lanes)
    payload = jnp.concatenate([split, cut.reshape(devices, window_rows, lanes)], axis=1)
    arrived = lax.all_to_all(payload, "dev", split_axis=0, concat_axis=0, tiled=True)
    rows0 = arrived[:, :state_rows]
    window0 = arrived[:, state_rows:].reshape(members, window_rows * lanes)[:, :window_size]
    window0 = window0.reshape(members, window_turbines, steps_count)
    per_row = output_linear_operator.reshape(tile_rows, lanes, steps_count)
    spread_operator = jnp.stack(
        [
            jnp.pad(per_row, ((j * tile_rows, (block_turbines - 1 - j) * tile_rows), (0, 0), (0, 0)))
            for j in range(block_turbines)
        ],
        axis=2,
    )
    rows1 = analysis(rows0, 0, window0)
    rows2 = analysis(rows1.reshape(members, state_rows * lanes), 1).reshape(members, block_turbines, rotor_line)
    back = lax.all_to_all(rows2, "dev", split_axis=0, concat_axis=0, tiled=True)
    return back.reshape(1, rotor_vectors, rotor_line)


def solution(mesh):
    return jax.shard_map(
        on_device,
        mesh=mesh,
        in_specs=(P("dev", None, None), P(), P(), P(), P(), P()),
        out_specs=P("dev", None, None),
        check_vma=False,
    )
```

```python
import math

import jax
import jax.numpy as jnp
from jax import lax
from jax.sharding import PartitionSpec as P

NSI = 6
HALO_REACH = 8


def block_weights(window, taper_bins, observed_window):
    members = window.shape[0]
    values = window.astype(jnp.float32)
    center = jnp.mean(values, axis=0)
    spread = values - center
    innovation = observed_window - center
    weighted = spread * taper_bins[None, :, None]
    flat_spread = spread.reshape(members, -1)
    flat_weighted = weighted.reshape(members, -1)
    gram = jnp.einsum("km,lm->kl", flat_weighted, flat_spread, precision=lax.Precision.HIGHEST)
    identity = jnp.eye(members, dtype=jnp.float32)
    system = (members - 1) * identity + gram
    scale = jnp.sqrt(jnp.sum(system * system))
    root = system / scale
    inverse = identity
    for sweep in range(NSI):
        middle = 1.5 * identity - 0.5 * jnp.dot(inverse, root, precision=lax.Precision.HIGHEST)
        both = jnp.einsum(
            "bkl,blm->bkm",
            jnp.stack([root, middle]),
            jnp.stack([middle, inverse]),
            precision=lax.Precision.HIGHEST,
        )
        root, inverse = both[0], both[1]
    inverse_root = inverse / jnp.sqrt(scale)
    pull = jnp.dot(flat_weighted, innovation.reshape(-1), precision=lax.Precision.HIGHEST)
    halfway = jnp.dot(inverse_root, pull, precision=lax.Precision.HIGHEST)
    offset = jnp.dot(inverse_root, halfway, precision=lax.Precision.HIGHEST)
    return math.sqrt(members - 1) * inverse_root + offset[:, None]


def ring_order(devices):
    if devices != 128:
        return list(range(devices))
    chips = []
    for z in range(4):
        ys = range(4) if z % 2 == 0 else range(3, -1, -1)
        for k, y in enumerate(ys):
            xs = range(4) if k % 2 == 0 else range(3, -1, -1)
            chips.extend((z, y, x) for x in xs)
    return [z * 32 + y * 8 + x * 2 + c for z, y, x in chips for c in range(2)]


def apply_weights(rows, weights):
    values = rows.astype(jnp.float32)
    center = jnp.mean(values, axis=0)
    spread = values - center
    moved = jnp.einsum("ik,i...->k...", weights, spread, precision=lax.Precision.HIGHEST)
    return (center + moved).astype(jnp.bfloat16)


def on_device(
    prior_trajectories,
    output_linear_operator,
    recorded_output,
    sensor_noise_spread,
    nearby_rotor_positions,
    cutoff_listing_amounts,
):
    _, rotor_vectors, rotor_line = prior_trajectories.shape
    blocks, width = nearby_rotor_positions.shape
    devices = lax.axis_size("dev")
    block_turbines = rotor_vectors // blocks
    members = devices
    steps_count = output_linear_operator.shape[1]
    ring = ring_order(devices)
    place = [0] * devices
    for p, d in enumerate(ring):
        place[d] = p
    me = jnp.asarray(place, dtype=jnp.int32)[lax.axis_index("dev")]
    first_turbine = me * block_turbines
    reach_blocks = -(-HALO_REACH // block_turbines)
    offsets = list(range(-reach_blocks, reach_blocks + 1))
    window_turbines = len(offsets) * block_turbines
    window_first = first_turbine - reach_blocks * block_turbines

    own_halo = lax.dynamic_index_in_dim(nearby_rotor_positions, me, 0, keepdims=False)
    own_counts = lax.dynamic_index_in_dim(cutoff_listing_amounts, me, 0, keepdims=False)
    window_ids = jnp.mod(window_first + jnp.arange(window_turbines, dtype=jnp.int32), rotor_vectors)
    relative = jnp.mod(own_halo - window_first, rotor_vectors)
    bins = (relative[:, None] == jnp.arange(window_turbines, dtype=jnp.int32)[None, :]).astype(
        jnp.float32
    )
    position = jnp.arange(width, dtype=jnp.float32)

    def taper_of(which):
        limit = own_counts[which].astype(jnp.float32)
        taper = jnp.where(position < limit, (1.0 - position / limit) ** 2, 0.0)
        weighting = taper / jnp.take(sensor_noise_spread[which], own_halo, axis=0)
        return jnp.sum(bins * weighting[:, None], axis=0)

    def observe_rows(rows):
        values = lax.dot_general(
            rows.reshape(members, state_rows, lanes),
            spread_operator,
            (((1, 2), (0, 1)), ((), ())),
            preferred_element_type=jnp.float32,
        )
        return values.astype(jnp.bfloat16).reshape(members, block_turbines, steps_count)

    def gather_window(own):
        pieces = []
        for o in offsets:
            if o == 0:
                pieces.append(own)
            else:
                pairs = [(ring[(p + o) % devices], ring[p]) for p in range(devices)]
                pieces.append(lax.ppermute(own, "dev", pairs))
        return jnp.concatenate(pieces, axis=1)

    def analysis(rows, which, window=None):
        if window is None:
            window = gather_window(observe_rows(rows))
        observed_window = jnp.take(recorded_output[which], window_ids, axis=0)
        weights = block_weights(window, taper_of(which), observed_window)
        return apply_weights(rows, weights)

    member_values = jnp.dot(
        prior_trajectories.reshape(rotor_vectors, rotor_line),
        output_linear_operator,
        preferred_element_type=jnp.float32,
    ).astype(jnp.bfloat16)
    placed = jnp.asarray(place, dtype=jnp.int32)
    source = jnp.mod(
        placed[:, None] * block_turbines
        - reach_blocks * block_turbines
        + jnp.arange(window_turbines, dtype=jnp.int32)[None, :],
        rotor_vectors,
    ).reshape(-1)
    pick = (source[:, None] == jnp.arange(rotor_vectors, dtype=jnp.int32)[None, :]).astype(jnp.bfloat16)
    cut = jnp.dot(pick, member_values, preferred_element_type=jnp.float32).astype(jnp.bfloat16)
    lanes = 128
    tile_rows = rotor_line // lanes
    state_rows = block_turbines * tile_rows
    window_size = window_turbines * steps_count
    window_rows = -(-window_size // lanes)
    cut = jnp.pad(cut.reshape(devices, window_size), ((0, 0), (0, window_rows * lanes - window_size)))
    split = jnp.take(prior_trajectories.reshape(devices, state_rows, lanes), placed, axis=0)
    payload = jnp.concatenate([split, cut.reshape(devices, window_rows, lanes)], axis=1)
    arrived = lax.all_to_all(payload, "dev", split_axis=0, concat_axis=0, tiled=True)
    rows0 = arrived[:, :state_rows]
    window0 = arrived[:, state_rows:].reshape(members, window_rows * lanes)[:, :window_size]
    window0 = window0.reshape(members, window_turbines, steps_count)
    per_row = output_linear_operator.reshape(tile_rows, lanes, steps_count)
    spread_operator = jnp.stack(
        [
            jnp.pad(per_row, ((j * tile_rows, (block_turbines - 1 - j) * tile_rows), (0, 0), (0, 0)))
            for j in range(block_turbines)
        ],
        axis=2,
    )
    rows1 = analysis(rows0, 0, window0)
    rows2 = analysis(rows1.reshape(members, state_rows * lanes), 1).reshape(members, block_turbines, rotor_line)
    back = lax.all_to_all(rows2, "dev", split_axis=0, concat_axis=0, tiled=True)
    back = jnp.take(back, jnp.asarray(ring, dtype=jnp.int32), axis=0)
    return back.reshape(1, rotor_vectors, rotor_line)


def solution(mesh):
    return jax.shard_map(
        on_device,
        mesh=mesh,
        in_specs=(P("dev", None, None), P(), P(), P(), P(), P()),
        out_specs=P("dev", None, None),
        check_vma=False,
    )
```

```python
import math

import jax
import jax.numpy as jnp
from jax import lax
from jax.sharding import PartitionSpec as P

NSI = 6
HALO_REACH = 8


def block_weights(window, taper_bins, observed_window):
    members = window.shape[0]
    values = window.astype(jnp.float32)
    center = jnp.mean(values, axis=0)
    spread = values - center
    innovation = observed_window - center
    weighted = spread * taper_bins[None, :, None]
    flat_spread = spread.reshape(members, -1)
    flat_weighted = weighted.reshape(members, -1)
    gram = jnp.einsum("km,lm->kl", flat_weighted, flat_spread, precision=lax.Precision.HIGHEST)
    identity = jnp.eye(members, dtype=jnp.float32)
    system = (members - 1) * identity + gram
    scale = jnp.sqrt(jnp.sum(system * system))
    root = system / scale
    inverse = identity
    for sweep in range(NSI):
        middle = 1.5 * identity - 0.5 * jnp.dot(inverse, root, precision=lax.Precision.HIGHEST)
        both = jnp.einsum(
            "bkl,blm->bkm",
            jnp.stack([root, middle]),
            jnp.stack([middle, inverse]),
            precision=lax.Precision.HIGHEST,
        )
        root, inverse = both[0], both[1]
    inverse_root = inverse / jnp.sqrt(scale)
    pull = jnp.dot(flat_weighted, innovation.reshape(-1), precision=lax.Precision.HIGHEST)
    halfway = jnp.dot(inverse_root, pull, precision=lax.Precision.HIGHEST)
    offset = jnp.dot(inverse_root, halfway, precision=lax.Precision.HIGHEST)
    return math.sqrt(members - 1) * inverse_root + offset[:, None]


def ring_order(devices):
    if devices != 128:
        return list(range(devices))
    chips = []
    for z in range(4):
        ys = range(4) if z % 2 == 0 else range(3, -1, -1)
        for k, y in enumerate(ys):
            xs = range(4) if k % 2 == 0 else range(3, -1, -1)
            chips.extend((z, y, x) for x in xs)
    return [z * 32 + y * 8 + x * 2 + c for z, y, x in chips for c in range(2)]


def in_block_order(received, ring):
    devices = received.shape[0]
    order = jnp.asarray(ring, dtype=jnp.int32)
    pick = (order[:, None] == jnp.arange(devices, dtype=jnp.int32)[None, :]).astype(received.dtype)
    flat = received.reshape(devices, -1)
    picked = jnp.dot(pick, flat, preferred_element_type=jnp.float32).astype(received.dtype)
    return picked.reshape(received.shape)


def apply_weights(rows, weights):
    values = rows.astype(jnp.float32)
    center = jnp.mean(values, axis=0)
    spread = values - center
    moved = jnp.einsum("ik,i...->k...", weights, spread, precision=lax.Precision.HIGHEST)
    return (center + moved).astype(jnp.bfloat16)


def on_device(
    prior_trajectories,
    output_linear_operator,
    recorded_output,
    sensor_noise_spread,
    nearby_rotor_positions,
    cutoff_listing_amounts,
):
    _, rotor_vectors, rotor_line = prior_trajectories.shape
    blocks, width = nearby_rotor_positions.shape
    devices = lax.axis_size("dev")
    block_turbines = rotor_vectors // blocks
    members = devices
    steps_count = output_linear_operator.shape[1]
    ring = ring_order(devices)
    place = [0] * devices
    for p, d in enumerate(ring):
        place[d] = p
    me = jnp.asarray(place, dtype=jnp.int32)[lax.axis_index("dev")]
    first_turbine = me * block_turbines
    reach_blocks = -(-HALO_REACH // block_turbines)
    offsets = list(range(-reach_blocks, reach_blocks + 1))
    window_turbines = len(offsets) * block_turbines
    window_first = first_turbine - reach_blocks * block_turbines

    own_halo = lax.dynamic_index_in_dim(nearby_rotor_positions, me, 0, keepdims=False)
    own_counts = lax.dynamic_index_in_dim(cutoff_listing_amounts, me, 0, keepdims=False)
    window_ids = jnp.mod(window_first + jnp.arange(window_turbines, dtype=jnp.int32), rotor_vectors)
    relative = jnp.mod(own_halo - window_first, rotor_vectors)
    bins = (relative[:, None] == jnp.arange(window_turbines, dtype=jnp.int32)[None, :]).astype(
        jnp.float32
    )
    position = jnp.arange(width, dtype=jnp.float32)

    def taper_of(which):
        limit = own_counts[which].astype(jnp.float32)
        taper = jnp.where(position < limit, (1.0 - position / limit) ** 2, 0.0)
        weighting = taper / jnp.take(sensor_noise_spread[which], own_halo, axis=0)
        return jnp.sum(bins * weighting[:, None], axis=0)

    def observe_rows(rows):
        values = lax.dot_general(
            rows.reshape(members, state_rows, lanes),
            spread_operator,
            (((1, 2), (0, 1)), ((), ())),
            preferred_element_type=jnp.float32,
        )
        return values.astype(jnp.bfloat16).reshape(members, block_turbines, steps_count)

    def gather_window(own):
        pieces = []
        for o in offsets:
            if o == 0:
                pieces.append(own)
            else:
                pairs = [(ring[(p + o) % devices], ring[p]) for p in range(devices)]
                pieces.append(lax.ppermute(own, "dev", pairs))
        return jnp.concatenate(pieces, axis=1)

    def analysis(rows, which, window=None):
        if window is None:
            window = gather_window(observe_rows(rows))
        observed_window = jnp.take(recorded_output[which], window_ids, axis=0)
        weights = block_weights(window, taper_of(which), observed_window)
        return apply_weights(rows, weights)

    member_values = jnp.dot(
        prior_trajectories.reshape(rotor_vectors, rotor_line),
        output_linear_operator,
        preferred_element_type=jnp.float32,
    ).astype(jnp.bfloat16)
    placed = jnp.asarray(place, dtype=jnp.int32)
    source = jnp.mod(
        placed[:, None] * block_turbines
        - reach_blocks * block_turbines
        + jnp.arange(window_turbines, dtype=jnp.int32)[None, :],
        rotor_vectors,
    ).reshape(-1)
    pick = (source[:, None] == jnp.arange(rotor_vectors, dtype=jnp.int32)[None, :]).astype(jnp.bfloat16)
    cut = jnp.dot(pick, member_values, preferred_element_type=jnp.float32).astype(jnp.bfloat16)
    lanes = 128
    tile_rows = rotor_line // lanes
    state_rows = block_turbines * tile_rows
    window_size = window_turbines * steps_count
    window_rows = -(-window_size // lanes)
    cut = jnp.pad(cut.reshape(devices, window_size), ((0, 0), (0, window_rows * lanes - window_size)))
    split = jnp.take(prior_trajectories.reshape(devices, state_rows, lanes), placed, axis=0)
    payload = jnp.concatenate([split, cut.reshape(devices, window_rows, lanes)], axis=1)
    arrived = lax.all_to_all(payload, "dev", split_axis=0, concat_axis=0, tiled=True)
    rows0 = arrived[:, :state_rows]
    window0 = arrived[:, state_rows:].reshape(members, window_rows * lanes)[:, :window_size]
    window0 = window0.reshape(members, window_turbines, steps_count)
    per_row = output_linear_operator.reshape(tile_rows, lanes, steps_count)
    spread_operator = jnp.stack(
        [
            jnp.pad(per_row, ((j * tile_rows, (block_turbines - 1 - j) * tile_rows), (0, 0), (0, 0)))
            for j in range(block_turbines)
        ],
        axis=2,
    )
    rows1 = analysis(rows0, 0, window0)
    rows2 = analysis(rows1.reshape(members, state_rows * lanes), 1).reshape(members, block_turbines, rotor_line)
    back = lax.all_to_all(rows2, "dev", split_axis=0, concat_axis=0, tiled=True)
    return in_block_order(back, ring).reshape(1, rotor_vectors, rotor_line)


def solution(mesh):
    return jax.shard_map(
        on_device,
        mesh=mesh,
        in_specs=(P("dev", None, None), P(), P(), P(), P(), P()),
        out_specs=P("dev", None, None),
        check_vma=False,
    )
```

```python
import math

import jax
import jax.numpy as jnp
from jax import lax
from jax.sharding import PartitionSpec as P

NSI = 6
HALO_REACH = 8


def block_weights(window, taper_bins, observed_window):
    members = window.shape[0]
    values = window.astype(jnp.float32)
    center = jnp.mean(values, axis=0)
    spread = values - center
    innovation = observed_window - center
    weighted = spread * taper_bins[None, :, None]
    flat_spread = spread.reshape(members, -1)
    flat_weighted = weighted.reshape(members, -1)
    gram = jnp.einsum("km,lm->kl", flat_weighted, flat_spread, precision=lax.Precision.HIGHEST)
    identity = jnp.eye(members, dtype=jnp.float32)
    system = (members - 1) * identity + gram
    scale = jnp.sqrt(jnp.sum(system * system))
    root = system / scale
    inverse = identity
    for sweep in range(NSI):
        middle = 1.5 * identity - 0.5 * jnp.dot(inverse, root, precision=lax.Precision.HIGHEST)
        both = jnp.einsum(
            "bkl,blm->bkm",
            jnp.stack([root, middle]),
            jnp.stack([middle, inverse]),
            precision=lax.Precision.HIGHEST,
        )
        root, inverse = both[0], both[1]
    inverse_root = inverse / jnp.sqrt(scale)
    pull = jnp.dot(flat_weighted, innovation.reshape(-1), precision=lax.Precision.HIGHEST)
    halfway = jnp.dot(inverse_root, pull, precision=lax.Precision.HIGHEST)
    offset = jnp.dot(inverse_root, halfway, precision=lax.Precision.HIGHEST)
    return math.sqrt(members - 1) * inverse_root + offset[:, None]


def ring_order(devices):
    if devices != 128:
        return list(range(devices))
    chips = []
    for z in range(4):
        ys = range(4) if z % 2 == 0 else range(3, -1, -1)
        for k, y in enumerate(ys):
            xs = range(4) if k % 2 == 0 else range(3, -1, -1)
            chips.extend((z, y, x) for x in xs)
    return [z * 32 + y * 8 + x * 2 + c for z, y, x in chips for c in range(2)]


def in_block_order(received, ring):
    devices = received.shape[0]
    order = jnp.asarray(ring, dtype=jnp.int32)
    pick = (order[:, None] == jnp.arange(devices, dtype=jnp.int32)[None, :]).astype(received.dtype)
    flat = received.reshape(devices, -1)
    picked = jnp.dot(pick, flat, preferred_element_type=jnp.float32).astype(received.dtype)
    return picked.reshape(received.shape)


def apply_weights(rows, weights):
    values = rows.astype(jnp.float32)
    center = jnp.mean(values, axis=0)
    spread = values - center
    moved = jnp.einsum("ik,i...->k...", weights, spread, precision=lax.Precision.HIGHEST)
    return (center + moved).astype(jnp.bfloat16)


def on_device(
    prior_trajectories,
    output_linear_operator,
    recorded_output,
    sensor_noise_spread,
    nearby_rotor_positions,
    cutoff_listing_amounts,
):
    _, rotor_vectors, rotor_line = prior_trajectories.shape
    blocks, width = nearby_rotor_positions.shape
    devices = lax.axis_size("dev")
    block_turbines = rotor_vectors // blocks
    members = devices
    steps_count = output_linear_operator.shape[1]
    ring = ring_order(devices)
    place = [0] * devices
    for p, d in enumerate(ring):
        place[d] = p
    me = jnp.asarray(place, dtype=jnp.int32)[lax.axis_index("dev")]
    first_turbine = me * block_turbines
    reach_blocks = -(-HALO_REACH // block_turbines)
    offsets = list(range(-reach_blocks, reach_blocks + 1))
    window_turbines = len(offsets) * block_turbines
    window_first = first_turbine - reach_blocks * block_turbines

    own_halo = lax.dynamic_index_in_dim(nearby_rotor_positions, me, 0, keepdims=False)
    own_counts = lax.dynamic_index_in_dim(cutoff_listing_amounts, me, 0, keepdims=False)
    window_ids = jnp.mod(window_first + jnp.arange(window_turbines, dtype=jnp.int32), rotor_vectors)
    relative = jnp.mod(own_halo - window_first, rotor_vectors)
    bins = (relative[:, None] == jnp.arange(window_turbines, dtype=jnp.int32)[None, :]).astype(
        jnp.float32
    )
    position = jnp.arange(width, dtype=jnp.float32)

    def taper_of(which):
        limit = own_counts[which].astype(jnp.float32)
        taper = jnp.where(position < limit, (1.0 - position / limit) ** 2, 0.0)
        weighting = taper / jnp.take(sensor_noise_spread[which], own_halo, axis=0)
        return jnp.sum(bins * weighting[:, None], axis=0)

    def observe_rows(rows):
        values = lax.dot_general(
            rows.reshape(members, state_rows, lanes),
            spread_operator,
            (((1, 2), (0, 1)), ((), ())),
            preferred_element_type=jnp.float32,
        )
        return values.astype(jnp.bfloat16).reshape(members, block_turbines, steps_count)

    def shifted(value, o):
        return lax.ppermute(value, "dev", [(ring[(p + o) % devices], ring[p]) for p in range(devices)])

    def gather_window(own):
        if reach_blocks == 4:
            near = jnp.concatenate([shifted(own, -1), own, shifted(own, 1)], axis=1)
            return jnp.concatenate([shifted(near, -3), near, shifted(near, 3)], axis=1)
        pieces = [own if o == 0 else shifted(own, o) for o in offsets]
        return jnp.concatenate(pieces, axis=1)

    def analysis(rows, which, window=None):
        if window is None:
            window = gather_window(observe_rows(rows))
        observed_window = jnp.take(recorded_output[which], window_ids, axis=0)
        weights = block_weights(window, taper_of(which), observed_window)
        return apply_weights(rows, weights)

    member_values = jnp.dot(
        prior_trajectories.reshape(rotor_vectors, rotor_line),
        output_linear_operator,
        preferred_element_type=jnp.float32,
    ).astype(jnp.bfloat16)
    placed = jnp.asarray(place, dtype=jnp.int32)
    source = jnp.mod(
        placed[:, None] * block_turbines
        - reach_blocks * block_turbines
        + jnp.arange(window_turbines, dtype=jnp.int32)[None, :],
        rotor_vectors,
    ).reshape(-1)
    pick = (source[:, None] == jnp.arange(rotor_vectors, dtype=jnp.int32)[None, :]).astype(jnp.bfloat16)
    cut = jnp.dot(pick, member_values, preferred_element_type=jnp.float32).astype(jnp.bfloat16)
    lanes = 128
    tile_rows = rotor_line // lanes
    state_rows = block_turbines * tile_rows
    window_size = window_turbines * steps_count
    window_rows = -(-window_size // lanes)
    cut = jnp.pad(cut.reshape(devices, window_size), ((0, 0), (0, window_rows * lanes - window_size)))
    split = jnp.take(prior_trajectories.reshape(devices, state_rows, lanes), placed, axis=0)
    payload = jnp.concatenate([split, cut.reshape(devices, window_rows, lanes)], axis=1)
    arrived = lax.all_to_all(payload, "dev", split_axis=0, concat_axis=0, tiled=True)
    rows0 = arrived[:, :state_rows]
    window0 = arrived[:, state_rows:].reshape(members, window_rows * lanes)[:, :window_size]
    window0 = window0.reshape(members, window_turbines, steps_count)
    per_row = output_linear_operator.reshape(tile_rows, lanes, steps_count)
    spread_operator = jnp.stack(
        [
            jnp.pad(per_row, ((j * tile_rows, (block_turbines - 1 - j) * tile_rows), (0, 0), (0, 0)))
            for j in range(block_turbines)
        ],
        axis=2,
    )
    rows1 = analysis(rows0, 0, window0)
    rows2 = analysis(rows1.reshape(members, state_rows * lanes), 1).reshape(members, block_turbines, rotor_line)
    back = lax.all_to_all(rows2, "dev", split_axis=0, concat_axis=0, tiled=True)
    return in_block_order(back, ring).reshape(1, rotor_vectors, rotor_line)


def solution(mesh):
    return jax.shard_map(
        on_device,
        mesh=mesh,
        in_specs=(P("dev", None, None), P(), P(), P(), P(), P()),
        out_specs=P("dev", None, None),
        check_vma=False,
    )
```

```python
import math

import jax
import jax.numpy as jnp
from jax import lax
from jax.sharding import PartitionSpec as P

NSI = 6
HALO_REACH = 8


def block_weights(window, taper_bins, observed_window):
    members = window.shape[0]
    values = window.astype(jnp.float32)
    center = jnp.mean(values, axis=0)
    spread = values - center
    innovation = observed_window - center
    weighted = spread * taper_bins[None, :, None]
    flat_spread = spread.reshape(members, -1)
    flat_weighted = weighted.reshape(members, -1)
    gram = jnp.einsum("km,lm->kl", flat_weighted, flat_spread, precision=lax.Precision.HIGHEST)
    identity = jnp.eye(members, dtype=jnp.float32)
    system = (members - 1) * identity + gram
    scale = jnp.sqrt(jnp.sum(system * system))
    root = system / scale
    inverse = identity
    for sweep in range(NSI):
        middle = 1.5 * identity - 0.5 * jnp.dot(inverse, root, precision=lax.Precision.HIGHEST)
        both = jnp.einsum(
            "bkl,blm->bkm",
            jnp.stack([root, middle]),
            jnp.stack([middle, inverse]),
            precision=lax.Precision.HIGHEST,
        )
        root, inverse = both[0], both[1]
    inverse_root = inverse / jnp.sqrt(scale)
    pull = jnp.dot(flat_weighted, innovation.reshape(-1), precision=lax.Precision.HIGHEST)
    halfway = jnp.dot(inverse_root, pull, precision=lax.Precision.HIGHEST)
    offset = jnp.dot(inverse_root, halfway, precision=lax.Precision.HIGHEST)
    return math.sqrt(members - 1) * inverse_root + offset[:, None]


def ring_order(devices):
    if devices != 128:
        return list(range(devices))
    chips = []
    for z in range(4):
        ys = range(4) if z % 2 == 0 else range(3, -1, -1)
        for k, y in enumerate(ys):
            xs = range(4) if k % 2 == 0 else range(3, -1, -1)
            chips.extend((z, y, x) for x in xs)
    return [z * 32 + y * 8 + x * 2 + c for z, y, x in chips for c in range(2)]


def in_block_order(received, ring):
    devices = received.shape[0]
    order = jnp.asarray(ring, dtype=jnp.int32)
    pick = (order[:, None] == jnp.arange(devices, dtype=jnp.int32)[None, :]).astype(received.dtype)
    flat = received.reshape(devices, -1)
    picked = jnp.dot(pick, flat, preferred_element_type=jnp.float32).astype(received.dtype)
    return picked.reshape(received.shape)


def apply_weights(rows, weights):
    values = rows.astype(jnp.float32)
    center = jnp.mean(values, axis=0)
    moved = jnp.einsum("ik,i...->k...", weights, values, precision=lax.Precision.HIGHEST)
    keep = 1.0 - jnp.sum(weights, axis=0)
    keep = keep.reshape(keep.shape + (1,) * (values.ndim - 1))
    return (moved + keep * center).astype(jnp.bfloat16)


def on_device(
    prior_trajectories,
    output_linear_operator,
    recorded_output,
    sensor_noise_spread,
    nearby_rotor_positions,
    cutoff_listing_amounts,
):
    _, rotor_vectors, rotor_line = prior_trajectories.shape
    blocks, width = nearby_rotor_positions.shape
    devices = lax.axis_size("dev")
    block_turbines = rotor_vectors // blocks
    members = devices
    steps_count = output_linear_operator.shape[1]
    ring = ring_order(devices)
    place = [0] * devices
    for p, d in enumerate(ring):
        place[d] = p
    me = jnp.asarray(place, dtype=jnp.int32)[lax.axis_index("dev")]
    first_turbine = me * block_turbines
    reach_blocks = -(-HALO_REACH // block_turbines)
    offsets = list(range(-reach_blocks, reach_blocks + 1))
    window_turbines = len(offsets) * block_turbines
    window_first = first_turbine - reach_blocks * block_turbines

    own_halo = lax.dynamic_index_in_dim(nearby_rotor_positions, me, 0, keepdims=False)
    own_counts = lax.dynamic_index_in_dim(cutoff_listing_amounts, me, 0, keepdims=False)
    window_ids = jnp.mod(window_first + jnp.arange(window_turbines, dtype=jnp.int32), rotor_vectors)
    relative = jnp.mod(own_halo - window_first, rotor_vectors)
    bins = (relative[:, None] == jnp.arange(window_turbines, dtype=jnp.int32)[None, :]).astype(
        jnp.float32
    )
    position = jnp.arange(width, dtype=jnp.float32)

    def taper_of(which):
        limit = own_counts[which].astype(jnp.float32)
        taper = jnp.where(position < limit, (1.0 - position / limit) ** 2, 0.0)
        weighting = taper / jnp.take(sensor_noise_spread[which], own_halo, axis=0)
        return jnp.sum(bins * weighting[:, None], axis=0)

    def observe_rows(rows):
        values = lax.dot_general(
            rows.reshape(members, state_rows, lanes),
            spread_operator,
            (((1, 2), (0, 1)), ((), ())),
            preferred_element_type=jnp.float32,
        )
        return values.astype(jnp.bfloat16).reshape(members, block_turbines, steps_count)

    def shifted(value, o):
        return lax.ppermute(value, "dev", [(ring[(p + o) % devices], ring[p]) for p in range(devices)])

    def gather_window(own):
        if reach_blocks == 4:
            near = jnp.concatenate([shifted(own, -1), own, shifted(own, 1)], axis=1)
            return jnp.concatenate([shifted(near, -3), near, shifted(near, 3)], axis=1)
        pieces = [own if o == 0 else shifted(own, o) for o in offsets]
        return jnp.concatenate(pieces, axis=1)

    def analysis(rows, which, window=None):
        if window is None:
            window = gather_window(observe_rows(rows))
        observed_window = jnp.take(recorded_output[which], window_ids, axis=0)
        weights = block_weights(window, taper_of(which), observed_window)
        return apply_weights(rows, weights)

    member_values = jnp.dot(
        prior_trajectories.reshape(rotor_vectors, rotor_line),
        output_linear_operator,
        preferred_element_type=jnp.float32,
    ).astype(jnp.bfloat16)
    placed = jnp.asarray(place, dtype=jnp.int32)
    source = jnp.mod(
        placed[:, None] * block_turbines
        - reach_blocks * block_turbines
        + jnp.arange(window_turbines, dtype=jnp.int32)[None, :],
        rotor_vectors,
    ).reshape(-1)
    pick = (source[:, None] == jnp.arange(rotor_vectors, dtype=jnp.int32)[None, :]).astype(jnp.bfloat16)
    cut = jnp.dot(pick, member_values, preferred_element_type=jnp.float32).astype(jnp.bfloat16)
    lanes = 128
    tile_rows = rotor_line // lanes
    state_rows = block_turbines * tile_rows
    window_size = window_turbines * steps_count
    window_rows = -(-window_size // lanes)
    cut = jnp.pad(cut.reshape(devices, window_size), ((0, 0), (0, window_rows * lanes - window_size)))
    split = jnp.take(prior_trajectories.reshape(devices, state_rows, lanes), placed, axis=0)
    payload = jnp.concatenate([split, cut.reshape(devices, window_rows, lanes)], axis=1)
    arrived = lax.all_to_all(payload, "dev", split_axis=0, concat_axis=0, tiled=True)
    rows0 = arrived[:, :state_rows]
    window0 = arrived[:, state_rows:].reshape(members, window_rows * lanes)[:, :window_size]
    window0 = window0.reshape(members, window_turbines, steps_count)
    per_row = output_linear_operator.reshape(tile_rows, lanes, steps_count)
    spread_operator = jnp.stack(
        [
            jnp.pad(per_row, ((j * tile_rows, (block_turbines - 1 - j) * tile_rows), (0, 0), (0, 0)))
            for j in range(block_turbines)
        ],
        axis=2,
    )
    rows1 = analysis(rows0, 0, window0)
    rows2 = analysis(rows1.reshape(members, state_rows * lanes), 1).reshape(members, block_turbines, rotor_line)
    back = lax.all_to_all(rows2, "dev", split_axis=0, concat_axis=0, tiled=True)
    return in_block_order(back, ring).reshape(1, rotor_vectors, rotor_line)


def solution(mesh):
    return jax.shard_map(
        on_device,
        mesh=mesh,
        in_specs=(P("dev", None, None), P(), P(), P(), P(), P()),
        out_specs=P("dev", None, None),
        check_vma=False,
    )
```

```python
import math

import jax
import jax.numpy as jnp
from jax import lax
from jax.sharding import PartitionSpec as P

NSI = 6
HALO_REACH = 8


def block_weights(window, taper_bins, observed_window):
    members = window.shape[0]
    values = window.astype(jnp.float32)
    center = jnp.mean(values, axis=0)
    spread = values - center
    innovation = observed_window - center
    weighted = spread * taper_bins[None, :, None]
    flat_spread = spread.reshape(members, -1)
    flat_weighted = weighted.reshape(members, -1)
    gram = jnp.einsum("km,lm->kl", flat_weighted, flat_spread, precision=lax.Precision.HIGHEST)
    identity = jnp.eye(members, dtype=jnp.float32)
    system = (members - 1) * identity + gram
    scale = jnp.sqrt(jnp.sum(system * system))
    root = system / scale
    middle = 1.5 * identity - 0.5 * root
    root = jnp.dot(root, middle, precision=lax.Precision.HIGHEST)
    inverse = middle
    for sweep in range(1, NSI):
        middle = 1.5 * identity - 0.5 * jnp.dot(inverse, root, precision=lax.Precision.HIGHEST)
        both = jnp.einsum(
            "bkl,blm->bkm",
            jnp.stack([root, middle]),
            jnp.stack([middle, inverse]),
            precision=lax.Precision.HIGHEST,
        )
        root, inverse = both[0], both[1]
    inverse_root = inverse / jnp.sqrt(scale)
    pull = jnp.dot(flat_weighted, innovation.reshape(-1), precision=lax.Precision.HIGHEST)
    halfway = jnp.dot(inverse_root, pull, precision=lax.Precision.HIGHEST)
    offset = jnp.dot(inverse_root, halfway, precision=lax.Precision.HIGHEST)
    return math.sqrt(members - 1) * inverse_root + offset[:, None]


def ring_order(devices):
    if devices != 128:
        return list(range(devices))
    chips = []
    for z in range(4):
        ys = range(4) if z % 2 == 0 else range(3, -1, -1)
        for k, y in enumerate(ys):
            xs = range(4) if k % 2 == 0 else range(3, -1, -1)
            chips.extend((z, y, x) for x in xs)
    return [z * 32 + y * 8 + x * 2 + c for z, y, x in chips for c in range(2)]


def in_block_order(received, ring):
    devices = received.shape[0]
    order = jnp.asarray(ring, dtype=jnp.int32)
    pick = (order[:, None] == jnp.arange(devices, dtype=jnp.int32)[None, :]).astype(received.dtype)
    flat = received.reshape(devices, -1)
    picked = jnp.dot(pick, flat, preferred_element_type=jnp.float32).astype(received.dtype)
    return picked.reshape(received.shape)


def apply_weights(rows, weights):
    values = rows.astype(jnp.float32)
    center = jnp.mean(values, axis=0)
    moved = jnp.einsum("ik,i...->k...", weights, values, precision=lax.Precision.HIGHEST)
    keep = 1.0 - jnp.sum(weights, axis=0)
    keep = keep.reshape(keep.shape + (1,) * (values.ndim - 1))
    return (moved + keep * center).astype(jnp.bfloat16)


def on_device(
    prior_trajectories,
    output_linear_operator,
    recorded_output,
    sensor_noise_spread,
    nearby_rotor_positions,
    cutoff_listing_amounts,
):
    _, rotor_vectors, rotor_line = prior_trajectories.shape
    blocks, width = nearby_rotor_positions.shape
    devices = lax.axis_size("dev")
    block_turbines = rotor_vectors // blocks
    members = devices
    steps_count = output_linear_operator.shape[1]
    ring = ring_order(devices)
    place = [0] * devices
    for p, d in enumerate(ring):
        place[d] = p
    me = jnp.asarray(place, dtype=jnp.int32)[lax.axis_index("dev")]
    first_turbine = me * block_turbines
    reach_blocks = -(-HALO_REACH // block_turbines)
    offsets = list(range(-reach_blocks, reach_blocks + 1))
    window_turbines = len(offsets) * block_turbines
    window_first = first_turbine - reach_blocks * block_turbines

    own_halo = lax.dynamic_index_in_dim(nearby_rotor_positions, me, 0, keepdims=False)
    own_counts = lax.dynamic_index_in_dim(cutoff_listing_amounts, me, 0, keepdims=False)
    window_ids = jnp.mod(window_first + jnp.arange(window_turbines, dtype=jnp.int32), rotor_vectors)
    relative = jnp.mod(own_halo - window_first, rotor_vectors)
    bins = (relative[:, None] == jnp.arange(window_turbines, dtype=jnp.int32)[None, :]).astype(
        jnp.float32
    )
    position = jnp.arange(width, dtype=jnp.float32)

    def taper_of(which):
        limit = own_counts[which].astype(jnp.float32)
        taper = jnp.where(position < limit, (1.0 - position / limit) ** 2, 0.0)
        weighting = taper / jnp.take(sensor_noise_spread[which], own_halo, axis=0)
        return jnp.sum(bins * weighting[:, None], axis=0)

    def observe_rows(rows):
        values = lax.dot_general(
            rows.reshape(members, state_rows, lanes),
            spread_operator,
            (((1, 2), (0, 1)), ((), ())),
            preferred_element_type=jnp.float32,
        )
        return values.astype(jnp.bfloat16).reshape(members, block_turbines, steps_count)

    def shifted(value, o):
        return lax.ppermute(value, "dev", [(ring[(p + o) % devices], ring[p]) for p in range(devices)])

    def gather_window(own):
        if reach_blocks == 4:
            near = jnp.concatenate([shifted(own, -1), own, shifted(own, 1)], axis=1)
            return jnp.concatenate([shifted(near, -3), near, shifted(near, 3)], axis=1)
        pieces = [own if o == 0 else shifted(own, o) for o in offsets]
        return jnp.concatenate(pieces, axis=1)

    def analysis(rows, which, window=None):
        if window is None:
            window = gather_window(observe_rows(rows))
        observed_window = jnp.take(recorded_output[which], window_ids, axis=0)
        weights = block_weights(window, taper_of(which), observed_window)
        return apply_weights(rows, weights)

    member_values = jnp.dot(
        prior_trajectories.reshape(rotor_vectors, rotor_line),
        output_linear_operator,
        preferred_element_type=jnp.float32,
    ).astype(jnp.bfloat16)
    placed = jnp.asarray(place, dtype=jnp.int32)
    source = jnp.mod(
        placed[:, None] * block_turbines
        - reach_blocks * block_turbines
        + jnp.arange(window_turbines, dtype=jnp.int32)[None, :],
        rotor_vectors,
    ).reshape(-1)
    pick = (source[:, None] == jnp.arange(rotor_vectors, dtype=jnp.int32)[None, :]).astype(jnp.bfloat16)
    cut = jnp.dot(pick, member_values, preferred_element_type=jnp.float32).astype(jnp.bfloat16)
    lanes = 128
    tile_rows = rotor_line // lanes
    state_rows = block_turbines * tile_rows
    window_size = window_turbines * steps_count
    window_rows = -(-window_size // lanes)
    cut = jnp.pad(cut.reshape(devices, window_size), ((0, 0), (0, window_rows * lanes - window_size)))
    split = jnp.take(prior_trajectories.reshape(devices, state_rows, lanes), placed, axis=0)
    payload = jnp.concatenate([split, cut.reshape(devices, window_rows, lanes)], axis=1)
    arrived = lax.all_to_all(payload, "dev", split_axis=0, concat_axis=0, tiled=True)
    rows0 = arrived[:, :state_rows]
    window0 = arrived[:, state_rows:].reshape(members, window_rows * lanes)[:, :window_size]
    window0 = window0.reshape(members, window_turbines, steps_count)
    per_row = output_linear_operator.reshape(tile_rows, lanes, steps_count)
    spread_operator = jnp.stack(
        [
            jnp.pad(per_row, ((j * tile_rows, (block_turbines - 1 - j) * tile_rows), (0, 0), (0, 0)))
            for j in range(block_turbines)
        ],
        axis=2,
    )
    rows1 = analysis(rows0, 0, window0)
    rows2 = analysis(rows1.reshape(members, state_rows * lanes), 1).reshape(members, block_turbines, rotor_line)
    back = lax.all_to_all(rows2, "dev", split_axis=0, concat_axis=0, tiled=True)
    return in_block_order(back, ring).reshape(1, rotor_vectors, rotor_line)


def solution(mesh):
    return jax.shard_map(
        on_device,
        mesh=mesh,
        in_specs=(P("dev", None, None), P(), P(), P(), P(), P()),
        out_specs=P("dev", None, None),
        check_vma=False,
    )
```

```python
import math

import jax
import jax.numpy as jnp
from jax import lax
from jax.sharding import PartitionSpec as P

NSI = 6
HALO_REACH = 8


def block_weights(window, taper_bins, observed_window):
    members = window.shape[0]
    values = window.astype(jnp.float32)
    center = jnp.mean(values, axis=0)
    spread = values - center
    innovation = observed_window - center
    weighted = spread * taper_bins[None, :, None]
    flat_spread = spread.reshape(members, -1)
    flat_weighted = weighted.reshape(members, -1)
    gram = jnp.einsum("km,lm->kl", flat_weighted, flat_spread, precision=lax.Precision.HIGHEST)
    identity = jnp.eye(members, dtype=jnp.float32)
    system = (members - 1) * identity + gram
    scale = jnp.sqrt(jnp.sum(system * system))
    root = system / scale
    middle = 1.5 * identity - 0.5 * root
    root = jnp.dot(root, middle, precision=lax.Precision.HIGHEST)
    inverse = middle
    for sweep in range(1, NSI):
        middle = 1.5 * identity - 0.5 * jnp.dot(inverse, root, precision=lax.Precision.HIGHEST)
        both = jnp.einsum(
            "bkl,blm->bkm",
            jnp.stack([root, middle]),
            jnp.stack([middle, inverse]),
            precision=lax.Precision.HIGHEST,
        )
        root, inverse = both[0], both[1]
    inverse_root = inverse / jnp.sqrt(scale)
    pull = jnp.dot(flat_weighted, innovation.reshape(-1), precision=lax.Precision.HIGHEST)
    halfway = jnp.dot(inverse_root, pull, precision=lax.Precision.HIGHEST)
    offset = jnp.dot(inverse_root, halfway, precision=lax.Precision.HIGHEST)
    return math.sqrt(members - 1) * inverse_root + offset[:, None]


def ring_order(devices):
    if devices != 128:
        return list(range(devices))
    chips = []
    for z in range(4):
        ys = range(4) if z % 2 == 0 else range(3, -1, -1)
        for k, y in enumerate(ys):
            xs = range(4) if k % 2 == 0 else range(3, -1, -1)
            chips.extend((z, y, x) for x in xs)
    return [z * 32 + y * 8 + x * 2 + c for z, y, x in chips for c in range(2)]


def in_block_order(received, ring):
    devices, parts, features = received.shape
    order = jnp.asarray(ring, dtype=jnp.int32)
    target = jnp.arange(devices * parts, dtype=jnp.int32)
    source = order[target // parts] * parts + target % parts
    pick = (source[:, None] == jnp.arange(devices * parts, dtype=jnp.int32)[None, :]).astype(received.dtype)
    flat = received.reshape(devices * parts, features)
    return jnp.dot(pick, flat, preferred_element_type=jnp.float32).astype(received.dtype)


def apply_weights(rows, weights):
    values = rows.astype(jnp.float32)
    center = jnp.mean(values, axis=0)
    moved = jnp.einsum("ik,i...->k...", weights, values, precision=lax.Precision.HIGHEST)
    keep = 1.0 - jnp.sum(weights, axis=0)
    keep = keep.reshape(keep.shape + (1,) * (values.ndim - 1))
    return (moved + keep * center).astype(jnp.bfloat16)


def on_device(
    prior_trajectories,
    output_linear_operator,
    recorded_output,
    sensor_noise_spread,
    nearby_rotor_positions,
    cutoff_listing_amounts,
):
    _, rotor_vectors, rotor_line = prior_trajectories.shape
    blocks, width = nearby_rotor_positions.shape
    devices = lax.axis_size("dev")
    block_turbines = rotor_vectors // blocks
    members = devices
    steps_count = output_linear_operator.shape[1]
    ring = ring_order(devices)
    place = [0] * devices
    for p, d in enumerate(ring):
        place[d] = p
    me = jnp.asarray(place, dtype=jnp.int32)[lax.axis_index("dev")]
    first_turbine = me * block_turbines
    reach_blocks = -(-HALO_REACH // block_turbines)
    offsets = list(range(-reach_blocks, reach_blocks + 1))
    window_turbines = len(offsets) * block_turbines
    window_first = first_turbine - reach_blocks * block_turbines

    own_halo = lax.dynamic_index_in_dim(nearby_rotor_positions, me, 0, keepdims=False)
    own_counts = lax.dynamic_index_in_dim(cutoff_listing_amounts, me, 0, keepdims=False)
    window_ids = jnp.mod(window_first + jnp.arange(window_turbines, dtype=jnp.int32), rotor_vectors)
    relative = jnp.mod(own_halo - window_first, rotor_vectors)
    bins = (relative[:, None] == jnp.arange(window_turbines, dtype=jnp.int32)[None, :]).astype(
        jnp.float32
    )
    position = jnp.arange(width, dtype=jnp.float32)

    def taper_of(which):
        limit = own_counts[which].astype(jnp.float32)
        taper = jnp.where(position < limit, (1.0 - position / limit) ** 2, 0.0)
        weighting = taper / jnp.take(sensor_noise_spread[which], own_halo, axis=0)
        return jnp.sum(bins * weighting[:, None], axis=0)

    def observe_rows(rows):
        values = lax.dot_general(
            rows.reshape(members, state_rows, lanes),
            spread_operator,
            (((1, 2), (0, 1)), ((), ())),
            preferred_element_type=jnp.float32,
        )
        return values.astype(jnp.bfloat16).reshape(members, block_turbines, steps_count)

    def shifted(value, o):
        return lax.ppermute(value, "dev", [(ring[(p + o) % devices], ring[p]) for p in range(devices)])

    def gather_window(own):
        if reach_blocks == 4:
            near = jnp.concatenate([shifted(own, -1), own, shifted(own, 1)], axis=1)
            return jnp.concatenate([shifted(near, -3), near, shifted(near, 3)], axis=1)
        pieces = [own if o == 0 else shifted(own, o) for o in offsets]
        return jnp.concatenate(pieces, axis=1)

    def analysis(rows, which, window=None):
        if window is None:
            window = gather_window(observe_rows(rows))
        observed_window = jnp.take(recorded_output[which], window_ids, axis=0)
        weights = block_weights(window, taper_of(which), observed_window)
        return apply_weights(rows, weights)

    member_values = jnp.dot(
        prior_trajectories.reshape(rotor_vectors, rotor_line),
        output_linear_operator,
        preferred_element_type=jnp.float32,
    ).astype(jnp.bfloat16)
    placed = jnp.asarray(place, dtype=jnp.int32)
    source = jnp.mod(
        placed[:, None] * block_turbines
        - reach_blocks * block_turbines
        + jnp.arange(window_turbines, dtype=jnp.int32)[None, :],
        rotor_vectors,
    ).reshape(-1)
    pick = (source[:, None] == jnp.arange(rotor_vectors, dtype=jnp.int32)[None, :]).astype(jnp.bfloat16)
    cut = jnp.dot(pick, member_values, preferred_element_type=jnp.float32).astype(jnp.bfloat16)
    lanes = 128
    tile_rows = rotor_line // lanes
    state_rows = block_turbines * tile_rows
    window_size = window_turbines * steps_count
    window_rows = -(-window_size // lanes)
    cut = jnp.pad(cut.reshape(devices, window_size), ((0, 0), (0, window_rows * lanes - window_size)))
    split = jnp.take(prior_trajectories.reshape(devices, state_rows, lanes), placed, axis=0)
    payload = jnp.concatenate([split, cut.reshape(devices, window_rows, lanes)], axis=1)
    arrived = lax.all_to_all(payload, "dev", split_axis=0, concat_axis=0, tiled=True)
    rows0 = arrived[:, :state_rows]
    window0 = arrived[:, state_rows:].reshape(members, window_rows * lanes)[:, :window_size]
    window0 = window0.reshape(members, window_turbines, steps_count)
    per_row = output_linear_operator.reshape(tile_rows, lanes, steps_count)
    spread_operator = jnp.stack(
        [
            jnp.pad(per_row, ((j * tile_rows, (block_turbines - 1 - j) * tile_rows), (0, 0), (0, 0)))
            for j in range(block_turbines)
        ],
        axis=2,
    )
    rows1 = analysis(rows0, 0, window0)
    rows2 = analysis(rows1.reshape(members, state_rows * lanes), 1).reshape(members, block_turbines, rotor_line)
    back = lax.all_to_all(rows2, "dev", split_axis=0, concat_axis=0, tiled=True)
    return in_block_order(back, ring).reshape(1, rotor_vectors, rotor_line)


def solution(mesh):
    return jax.shard_map(
        on_device,
        mesh=mesh,
        in_specs=(P("dev", None, None), P(), P(), P(), P(), P()),
        out_specs=P("dev", None, None),
        check_vma=False,
    )
```

```python
import math

import jax
import jax.numpy as jnp
from jax import lax
from jax.sharding import PartitionSpec as P

NSI = 6
HALO_REACH = 8


def block_weights(window, taper_bins, observed_window):
    members = window.shape[0]
    values = window.astype(jnp.float32)
    center = jnp.mean(values, axis=0)
    spread = values - center
    innovation = observed_window - center
    weighted = spread * taper_bins[None, :, None]
    flat_spread = spread.reshape(members, -1)
    flat_weighted = weighted.reshape(members, -1)
    gram = jnp.einsum("km,lm->kl", flat_weighted, flat_spread, precision=lax.Precision.HIGHEST)
    identity = jnp.eye(members, dtype=jnp.float32)
    system = (members - 1) * identity + gram
    scale = jnp.sqrt(jnp.sum(system * system))
    root = system / scale
    middle = 1.5 * identity - 0.5 * root
    root = jnp.dot(root, middle, precision=lax.Precision.HIGHEST)
    inverse = middle
    for sweep in range(1, NSI):
        middle = 1.5 * identity - 0.5 * jnp.dot(inverse, root, precision=lax.Precision.HIGHEST)
        both = jnp.einsum(
            "bkl,blm->bkm",
            jnp.stack([root, middle]),
            jnp.stack([middle, inverse]),
            precision=lax.Precision.HIGHEST,
        )
        root, inverse = both[0], both[1]
    inverse_root = inverse / jnp.sqrt(scale)
    pull = jnp.dot(flat_weighted, innovation.reshape(-1), precision=lax.Precision.HIGHEST)
    halfway = jnp.dot(inverse_root, pull, precision=lax.Precision.HIGHEST)
    offset = jnp.dot(inverse_root, halfway, precision=lax.Precision.HIGHEST)
    return math.sqrt(members - 1) * inverse_root + offset[:, None]


def ring_order(devices):
    if devices != 128:
        return list(range(devices))
    chips = []
    for z in range(4):
        ys = range(4) if z % 2 == 0 else range(3, -1, -1)
        for k, y in enumerate(ys):
            xs = range(4) if k % 2 == 0 else range(3, -1, -1)
            chips.extend((z, y, x) for x in xs)
    return [z * 32 + y * 8 + x * 2 + c for z, y, x in chips for c in range(2)]


def in_block_order(received, ring):
    devices = received.shape[0]
    order = jnp.asarray(ring, dtype=jnp.int32)
    pick = (order[:, None] == jnp.arange(devices, dtype=jnp.int32)[None, :]).astype(received.dtype)
    flat = received.reshape(devices, -1)
    picked = jnp.dot(pick, flat, preferred_element_type=jnp.float32).astype(received.dtype)
    return picked.reshape(received.shape)


def apply_weights(rows, weights):
    values = rows.astype(jnp.float32)
    center = jnp.mean(values, axis=0)
    moved = jnp.einsum("ik,i...->k...", weights, values, precision=lax.Precision.HIGHEST)
    keep = 1.0 - jnp.sum(weights, axis=0)
    keep = keep.reshape(keep.shape + (1,) * (values.ndim - 1))
    return (moved + keep * center).astype(jnp.bfloat16)


def on_device(
    prior_trajectories,
    output_linear_operator,
    recorded_output,
    sensor_noise_spread,
    nearby_rotor_positions,
    cutoff_listing_amounts,
):
    _, rotor_vectors, rotor_line = prior_trajectories.shape
    blocks, width = nearby_rotor_positions.shape
    devices = lax.axis_size("dev")
    block_turbines = rotor_vectors // blocks
    members = devices
    steps_count = output_linear_operator.shape[1]
    ring = ring_order(devices)
    place = [0] * devices
    for p, d in enumerate(ring):
        place[d] = p
    me = jnp.asarray(place, dtype=jnp.int32)[lax.axis_index("dev")]
    first_turbine = me * block_turbines
    reach_blocks = -(-HALO_REACH // block_turbines)
    offsets = list(range(-reach_blocks, reach_blocks + 1))
    window_turbines = len(offsets) * block_turbines
    window_first = first_turbine - reach_blocks * block_turbines

    own_halo = lax.dynamic_index_in_dim(nearby_rotor_positions, me, 0, keepdims=False)
    own_counts = lax.dynamic_index_in_dim(cutoff_listing_amounts, me, 0, keepdims=False)
    window_ids = jnp.mod(window_first + jnp.arange(window_turbines, dtype=jnp.int32), rotor_vectors)
    relative = jnp.mod(own_halo - window_first, rotor_vectors)
    bins = (relative[:, None] == jnp.arange(window_turbines, dtype=jnp.int32)[None, :]).astype(
        jnp.float32
    )
    position = jnp.arange(width, dtype=jnp.float32)

    def taper_of(which):
        limit = own_counts[which].astype(jnp.float32)
        taper = jnp.where(position < limit, (1.0 - position / limit) ** 2, 0.0)
        weighting = taper / jnp.take(sensor_noise_spread[which], own_halo, axis=0)
        return jnp.sum(bins * weighting[:, None], axis=0)

    def observe_rows(rows):
        values = lax.dot_general(
            rows.reshape(members, state_rows, lanes),
            spread_operator,
            (((1, 2), (0, 1)), ((), ())),
            preferred_element_type=jnp.float32,
        )
        return values.astype(jnp.bfloat16).reshape(members, block_turbines, steps_count)

    def shifted(value, o):
        return lax.ppermute(value, "dev", [(ring[(p + o) % devices], ring[p]) for p in range(devices)])

    def gather_window(own):
        if reach_blocks == 4:
            near = jnp.concatenate([shifted(own, -1), own, shifted(own, 1)], axis=1)
            return jnp.concatenate([shifted(near, -3), near, shifted(near, 3)], axis=1)
        pieces = [own if o == 0 else shifted(own, o) for o in offsets]
        return jnp.concatenate(pieces, axis=1)

    def analysis(rows, which, window=None):
        if window is None:
            window = gather_window(observe_rows(rows))
        observed_window = jnp.take(recorded_output[which], window_ids, axis=0)
        weights = block_weights(window, taper_of(which), observed_window)
        return apply_weights(rows, weights)

    member_values = jnp.dot(
        prior_trajectories.reshape(rotor_vectors, rotor_line),
        output_linear_operator,
        preferred_element_type=jnp.float32,
    ).astype(jnp.bfloat16)
    placed = jnp.asarray(place, dtype=jnp.int32)
    source = jnp.mod(
        placed[:, None] * block_turbines
        - reach_blocks * block_turbines
        + jnp.arange(window_turbines, dtype=jnp.int32)[None, :],
        rotor_vectors,
    ).reshape(-1)
    pick = (source[:, None] == jnp.arange(rotor_vectors, dtype=jnp.int32)[None, :]).astype(jnp.bfloat16)
    cut = jnp.dot(pick, member_values, preferred_element_type=jnp.float32).astype(jnp.bfloat16)
    lanes = 128
    tile_rows = rotor_line // lanes
    state_rows = block_turbines * tile_rows
    window_size = window_turbines * steps_count
    window_rows = -(-window_size // lanes)
    cut = jnp.pad(cut.reshape(devices, window_size), ((0, 0), (0, window_rows * lanes - window_size)))
    row_ids = jnp.arange(rotor_vectors, dtype=jnp.int32)
    row_source = placed[row_ids // block_turbines] * block_turbines + row_ids % block_turbines
    row_pick = (row_source[:, None] == row_ids[None, :]).astype(jnp.bfloat16)
    moved_rows = jnp.dot(
        row_pick, prior_trajectories.reshape(rotor_vectors, rotor_line), preferred_element_type=jnp.float32
    ).astype(jnp.bfloat16)
    split = moved_rows.reshape(devices, state_rows, lanes)
    payload = jnp.concatenate([split, cut.reshape(devices, window_rows, lanes)], axis=1)
    arrived = lax.all_to_all(payload, "dev", split_axis=0, concat_axis=0, tiled=True)
    rows0 = arrived[:, :state_rows]
    window0 = arrived[:, state_rows:].reshape(members, window_rows * lanes)[:, :window_size]
    window0 = window0.reshape(members, window_turbines, steps_count)
    per_row = output_linear_operator.reshape(tile_rows, lanes, steps_count)
    spread_operator = jnp.stack(
        [
            jnp.pad(per_row, ((j * tile_rows, (block_turbines - 1 - j) * tile_rows), (0, 0), (0, 0)))
            for j in range(block_turbines)
        ],
        axis=2,
    )
    rows1 = analysis(rows0, 0, window0)
    rows2 = analysis(rows1.reshape(members, state_rows * lanes), 1).reshape(members, block_turbines, rotor_line)
    back = lax.all_to_all(rows2, "dev", split_axis=0, concat_axis=0, tiled=True)
    return in_block_order(back, ring).reshape(1, rotor_vectors, rotor_line)


def solution(mesh):
    return jax.shard_map(
        on_device,
        mesh=mesh,
        in_specs=(P("dev", None, None), P(), P(), P(), P(), P()),
        out_specs=P("dev", None, None),
        check_vma=False,
    )
```
